32 devices in a mesh: leaf: 8 (over z, y), rhs: 4 (over x, core).
Axes of the slice: x: 2, y: 2, z: 4, core: 2. Of those that a mesh axis runs over, the one named last changes fastest.
Arguments:
- leaf_right: float32 [256, 256, 128], P('leaf', 'rhs'), may hold values from -6 to 6
- upper_right: float32 [16, 256, 128], P('leaf', 'rhs'), may hold values from -6 to 6
- leaf_inverse: bfloat16 [256, 128, 128], P(('leaf', 'rhs')), as said below
- upper_inverse: bfloat16 [16, 128, 128], P('leaf'), as said below
- update_blocks: bfloat16 [2048, 128, 128], P('leaf'), may hold values from -0.046875 to 0.046875
- block_target: int32 [2048, 1], P('leaf'), may hold values from 0 to 15; in each aligned block of 256 rows (0 to 255, 256 to 511, ...) at most 18 rows name the same one
- upper_place: int32 [16], replicated, may hold values from 0 to 15, each once
Outputs:
- leaf_solution: float32 [256, 256, 128], P('leaf', 'rhs')
- upper_solution: float32 [16, 256, 128], P('leaf', 'rhs')
The draws below stay inside these ranges and needn't reach their ends.
Inputs may be any that keep to these rules, and one draw needn't show every extreme that they name: `leaf_inverse`: lower triangular blocks, diagonal entries between 0.6 and 1.4. `upper_inverse`: lower triangular blocks, diagonal entries between 0.6 and 1.4. `block_target`: among the 256 blocks of one device no upper supernode is named more than 18 times, a bound that some block reaches. `upper_place`: each row of the upper arrays holds exactly one upper supernode.
All inputs are finite; a program needn't handle non-finite values.
Results may differ from the reference program's by a relative error of at most 0.0049.
Values may be sent and summed in bfloat16 or wider, within the bound.
No kernel may reach another device: no remote copies, remote signals or barrier semaphores. Data moves between devices by JAX's collectives and lax.ppermute only.
A program may use at most 64 MiB of HBM per device.

```python
import math
import jax
import jax.numpy as jnp
import numpy as np
from jax import lax

W = 128
RHS = 256
B = 8
S0 = 32
S1 = 2
N0 = 256
NS1 = 16
CAP = 18
N_LEAF = 8


def triangle_blocks(key, number):
    lower_key, diagonal_key = jax.random.split(key)
    lower = jax.random.normal(lower_key, (number, W, W), jnp.float32)
    lower = lower * (0.8 * W ** (-0.5))
    diagonal = jax.random.uniform(diagonal_key, (number, W), jnp.float32, 0.6, 1.4)
    row_index = jnp.arange(W)[:, None]
    column_index = jnp.arange(W)[None, :]
    below = row_index > column_index
    on_diagonal = row_index == column_index
    block = jnp.where(below[None], lower, 0.0) + jnp.where(on_diagonal[None], diagonal[:, :, None], 0.0)
    return block.astype(jnp.bfloat16)


def draw_leaf_inverse(key, part):
    return triangle_blocks(jax.random.fold_in(key, 11), N0)


def draw_upper_inverse(key, part):
    return triangle_blocks(jax.random.fold_in(key, 23), NS1)


def steps_of(stream_key, dims, cuts, smallest, high):
    factor_of = 1.0
    for dim, parts in cuts:
        heights = jax.random.uniform(jax.random.fold_in(jax.random.fold_in(stream_key, 6), dim), (parts,), jnp.float32, smallest / len(cuts), high / len(cuts))
        factor_of = factor_of * jnp.repeat(jnp.exp(heights), dims[dim] // parts).reshape((-1,) + (1,) * (len(dims) - 1 - dim))
    return factor_of


def assign_block(stream_key, own, number, rows, count, top, most, skew):
    order = jax.random.permutation(stream_key, count)
    packed, ordinary = portions_of(count, rows * top, most, skew, True), portions_of(count, rows * top, most, skew, False)
    places = jnp.arange(count)

    def named(lengths, offset_by):
        used = int((lengths > 0).sum())
        fixed = max(1, used // 4)
        passed = fixed + (places - fixed + offset_by * (used - fixed)) % max(1, count - fixed)
        return jnp.zeros((count,), jnp.int32).at[order[jnp.where(places < fixed, places, passed)]].set(jnp.asarray(lengths, jnp.int32))

    lengths = jnp.where(number % 4 == 0, named(packed, number // 4), named(ordinary, number - number // 4 - 1))
    mixed = jax.random.permutation(jax.random.fold_in(own, 3), count)
    source_of, sink = mixed[0:count // 2 * 2:2], mixed[1:count // 2 * 2:2]
    margin = jnp.minimum(lengths[source_of] - 1, most - lengths[sink]) // 2
    margin = jnp.where((source_of == order[0]) | (sink == order[0]) | (lengths[sink] == 0), 0, jnp.maximum(margin, 0))
    passed = jax.random.randint(jax.random.fold_in(own, 4), (count // 2,), 0, 1 << 20) % (margin + 1)
    lengths = lengths.at[source_of].add(-passed).at[sink].add(passed)
    items = jnp.searchsorted(jnp.cumsum(lengths), jnp.arange(rows * top), side="right").astype(jnp.int32)
    listing = items.reshape(top, rows).T
    listing = listing[jax.random.permutation(jax.random.fold_in(own, 1), rows)]
    offset_by = jax.random.randint(jax.random.fold_in(own, 2), (rows, 1), 0, top)
    return jnp.take_along_axis(listing, (jnp.arange(top)[None, :] + offset_by) % top, axis=1)


def portions_of(number_of, total, reach, slope, full):
    loads = [(1 << 20) // math.isqrt(rank ** slope) + 1 for rank in range(1, number_of + 1)]
    largest = reach if full else min(reach, max(-(-total // number_of), total * loads[0] // sum(loads)))
    least = 1 if total - largest >= number_of - 1 else 0
    holding, rest = [largest] + [least] * (number_of - 1), total - largest - least * (number_of - 1)
    while rest > 0:
        movable = [i for i in range(1, number_of) if holding[i] < largest] or [i for i in range(1, number_of) if holding[i] < reach]
        pool, budget = sum([loads[i] for i in movable]), rest
        for i in movable:
            more = min(reach - holding[i], max(1, budget * loads[i] // pool), rest)
            holding[i] = holding[i] + more
            rest = rest - more
    return np.array(holding)


def gaussian(rng, shape, spread, bound, cuts=(), kind=jnp.bfloat16):
    array = spread * jax.random.normal(rng, shape, jnp.float32)
    if cuts:
        array = array * steps_of(rng, shape, cuts, -0.22, 0.18)
    return jnp.clip(array, -bound, bound).astype(kind)


def setup_inputs(seed: int = 0) -> dict:
    key_of = jax.random.split(jax.random.key(seed), 8)
    leaf_right = gaussian(key_of[0], (N0, RHS, W), 1.0, 6.0, ((0, 8), (1, 4)), jnp.float32)
    upper_right = gaussian(key_of[1], (NS1, RHS, W), 1.0, 6.0, ((0, 8), (1, 4)), jnp.float32)
    leaf_inverse = draw_leaf_inverse(jax.random.fold_in(key_of[7], 71), 0)
    upper_inverse = draw_upper_inverse(jax.random.fold_in(key_of[7], 71), 0)
    update_blocks = gaussian(key_of[4], (N0 * B, W, W), (W * S0 * B // S1) ** -0.5, 0.046875, ((0, 8),))
    block_target_keys = jax.random.split(jax.random.fold_in(key_of[5], 1), (N0 * B) // (S0 * B))
    block_target_turns = jax.random.permutation(jax.random.fold_in(key_of[5], 3), (N0 * B) // (S0 * B))
    block_target = jax.vmap(lambda own, number: assign_block(jax.random.fold_in(key_of[5], 2), own, number, S0 * B, NS1, 1, CAP, 2))(block_target_keys, block_target_turns).reshape((N0 * B, 1))
    upper_place = jax.random.permutation(key_of[6], NS1).astype(jnp.int32)
    return {"leaf_right": leaf_right, "upper_right": upper_right, "leaf_inverse": leaf_inverse, "upper_inverse": upper_inverse, "update_blocks": update_blocks, "block_target": block_target, "upper_place": upper_place}


def to_half(values):
    return lax.optimization_barrier(values.astype(jnp.bfloat16)).astype(jnp.float32)


def reference(leaf_right, upper_right, leaf_inverse, upper_inverse, update_blocks, block_target, upper_place):
    inverse_wide = leaf_inverse.astype(jnp.float32)
    leaf_rounded = to_half(leaf_right)
    leaf_forward = jnp.einsum('ncw,nvw->ncv', leaf_rounded, inverse_wide)
    leaf_half = to_half(leaf_forward)
    position = upper_place[block_target[:, 0]].astype(jnp.int32)
    span_ids = jnp.arange(N_LEAF, dtype=jnp.int32)

    def forward_span(total, index):
        solved = lax.dynamic_slice_in_dim(leaf_half, index * S0, S0, 0)
        blocks = lax.dynamic_slice_in_dim(update_blocks, index * S0 * B, S0 * B, 0).astype(jnp.float32)
        blocks = blocks.reshape(S0, B, W, W)
        where_to = lax.dynamic_slice_in_dim(position, index * S0 * B, S0 * B, 0)
        terms = jnp.einsum('ncw,nbvw->nbcv', solved, blocks).reshape(S0 * B, RHS, W)
        return total + jax.ops.segment_sum(terms, where_to, num_segments=NS1), None

    upper_sums, unused = lax.scan(forward_span, jnp.zeros((NS1, RHS, W), jnp.float32), span_ids)
    upper_rounded = to_half(upper_right - upper_sums)
    upper_wide = upper_inverse.astype(jnp.float32)
    upper_half = to_half(jnp.einsum('pcw,pvw->pcv', upper_rounded, upper_wide))
    upper_solution = jnp.einsum('pcw,pwv->pcv', upper_half, upper_wide)
    upper_sent = to_half(upper_solution)

    def backward_span(index):
        where_to = lax.dynamic_slice_in_dim(position, index * S0 * B, S0 * B, 0)
        chosen = upper_sent[where_to]
        blocks = lax.dynamic_slice_in_dim(update_blocks, index * S0 * B, S0 * B, 0).astype(jnp.float32)
        corrections = jnp.einsum('kcv,kvw->kcw', chosen, blocks).reshape(S0, B, RHS, W).sum(axis=1)
        solved = lax.dynamic_slice_in_dim(leaf_forward, index * S0, S0, 0)
        leaf_back = to_half(solved - corrections)
        inverse_part = lax.dynamic_slice_in_dim(inverse_wide, index * S0, S0, 0)
        return jnp.einsum('ncw,nwv->ncv', leaf_back, inverse_part)

    leaf_solution = lax.map(backward_span, span_ids).reshape(N0, RHS, W)
    return leaf_solution, upper_solution
```

```python
import functools

import jax
import jax.numpy as jnp
from jax import lax
from jax.experimental import pallas as pl
from jax.experimental.pallas import tpu as pltpu
from jax.sharding import PartitionSpec as P

F32 = jnp.float32
BF16 = jnp.bfloat16
NT = (((1,), (1,)), ((), ()))
NN = (((1,), (0,)), ((), ()))


def _group(count):
    for g in (4, 2, 1):
        if count % g == 0:
            return g
    return 1


def forward_kernel(group, per_leaf, target_ref, place_ref, right_ref, inv_ref, blk_ref, fwd_ref, sums_ref):
    i = pl.program_id(0)

    @pl.when(i == 0)
    def _():
        sums_ref[...] = jnp.zeros_like(sums_ref)

    for g in range(group):
        rounded = right_ref[g].astype(BF16)
        forward = lax.dot_general(rounded, inv_ref[g], NT, preferred_element_type=F32)
        fwd_ref[g] = forward
        half = forward.astype(BF16)
        for b in range(per_leaf):
            k = (i * group + g) * per_leaf + b
            p = place_ref[target_ref[k]]
            term = lax.dot_general(half, blk_ref[g * per_leaf + b], NT, preferred_element_type=F32)
            sums_ref[p] += term


def backward_kernel(group, per_leaf, target_ref, place_ref, sent_ref, fwd_ref, inv_ref, blk_ref, out_ref):
    i = pl.program_id(0)
    for g in range(group):
        corr = None
        for b in range(per_leaf):
            k = (i * group + g) * per_leaf + b
            p = place_ref[target_ref[k]]
            term = lax.dot_general(sent_ref[p], blk_ref[g * per_leaf + b], NN, preferred_element_type=F32)
            corr = term if corr is None else corr + term
        back = (fwd_ref[g] - corr).astype(BF16)
        out_ref[g] = lax.dot_general(back, inv_ref[g], NN, preferred_element_type=F32)


def on_device(
    leaf_right, upper_right, leaf_inverse, upper_inverse, update_blocks, block_target, upper_place
):
    inverse_mine = lax.all_gather(leaf_inverse, "rhs", axis=0, tiled=True)
    leaf_count, columns, width = leaf_right.shape
    block_count = update_blocks.shape[0]
    per_leaf = block_count // leaf_count
    upper_total = upper_place.shape[0]
    group = _group(leaf_count)
    steps = leaf_count // group
    target = block_target.reshape(block_count)
    place = upper_place.astype(jnp.int32)
    params = pltpu.CompilerParams(
        dimension_semantics=("arbitrary",), vmem_limit_bytes=48 * 1024 * 1024
    )

    fwd_flops = 2 * leaf_count * columns * width * width * (1 + per_leaf)
    leaf_forward, sums = pl.pallas_call(
        functools.partial(forward_kernel, group, per_leaf),
        grid_spec=pltpu.PrefetchScalarGridSpec(
            num_scalar_prefetch=2,
            grid=(steps,),
            in_specs=[
                pl.BlockSpec((group, columns, width), lambda i, t, q: (i, 0, 0)),
                pl.BlockSpec((group, width, width), lambda i, t, q: (i, 0, 0)),
                pl.BlockSpec((group * per_leaf, width, width), lambda i, t, q: (i, 0, 0)),
            ],
            out_specs=[
                pl.BlockSpec((group, columns, width), lambda i, t, q: (i, 0, 0)),
                pl.BlockSpec((upper_total, columns, width), lambda i, t, q: (0, 0, 0)),
            ],
        ),
        out_shape=[
            jax.ShapeDtypeStruct((leaf_count, columns, width), F32),
            jax.ShapeDtypeStruct((upper_total, columns, width), F32),
        ],
        compiler_params=params,
        cost_estimate=pl.CostEstimate(
            flops=fwd_flops,
            transcendentals=0,
            bytes_accessed=update_blocks.size * 2 + leaf_right.size * 8 + inverse_mine.size * 2,
        ),
    )(target, place, leaf_right, inverse_mine, update_blocks)

    own = lax.psum_scatter(sums, "leaf", scatter_dimension=0, tiled=True)
    upper_rounded = (upper_right - own).astype(BF16)
    upper_half = jnp.einsum(
        "pcw,pvw->pcv", upper_rounded, upper_inverse, preferred_element_type=F32
    ).astype(BF16)
    upper_solution = jnp.einsum(
        "pcw,pwv->pcv", upper_half, upper_inverse, preferred_element_type=F32
    )
    sent_all = lax.all_gather(upper_solution.astype(BF16), "leaf", axis=0, tiled=True)

    leaf_solution = pl.pallas_call(
        functools.partial(backward_kernel, group, per_leaf),
        grid_spec=pltpu.PrefetchScalarGridSpec(
            num_scalar_prefetch=2,
            grid=(steps,),
            in_specs=[
                pl.BlockSpec((upper_total, columns, width), lambda i, t, q: (0, 0, 0)),
                pl.BlockSpec((group, columns, width), lambda i, t, q: (i, 0, 0)),
                pl.BlockSpec((group, width, width), lambda i, t, q: (i, 0, 0)),
                pl.BlockSpec((group * per_leaf, width, width), lambda i, t, q: (i, 0, 0)),
            ],
            out_specs=pl.BlockSpec((group, columns, width), lambda i, t, q: (i, 0, 0)),
        ),
        out_shape=jax.ShapeDtypeStruct((leaf_count, columns, width), F32),
        compiler_params=params,
        cost_estimate=pl.CostEstimate(
            flops=fwd_flops,
            transcendentals=0,
            bytes_accessed=update_blocks.size * 2 + leaf_right.size * 8 + inverse_mine.size * 2,
        ),
    )(target, place, sent_all, leaf_forward, inverse_mine, update_blocks)
    return (leaf_solution, upper_solution)


def solution(mesh):
    return jax.shard_map(
        on_device,
        mesh=mesh,
        in_specs=(
            P("leaf", "rhs", None),
            P("leaf", "rhs", None),
            P(("leaf", "rhs"), None, None),
            P("leaf", None, None),
            P("leaf", None, None),
            P("leaf", None),
            P(),
        ),
        out_specs=(P("leaf", "rhs", None), P("leaf", "rhs", None)),
        check_vma=False,
    )
```

```python
import functools

import jax
import jax.numpy as jnp
from jax import lax
from jax.experimental import pallas as pl
from jax.experimental.pallas import tpu as pltpu
from jax.sharding import PartitionSpec as P

F32 = jnp.float32
BF16 = jnp.bfloat16
NT = (((1,), (1,)), ((), ()))
NN = (((1,), (0,)), ((), ()))


def _group(count):
    for g in (4, 2, 1):
        if count % g == 0:
            return g
    return 1


def forward_kernel(group, per_leaf, target_ref, place_ref, r_ref, right_ref, inv_ref, blk_ref, fwd_ref, sums_ref):
    i = pl.program_id(0)

    @pl.when(i == 0)
    def _():
        sums_ref[...] = jnp.zeros_like(sums_ref)

    for g in range(group):
        rounded = right_ref[g].astype(BF16)
        forward = lax.dot_general(rounded, inv_ref[g], NT, preferred_element_type=F32)
        fwd_ref[g] = forward
        half = forward.astype(BF16)
        for b in range(per_leaf):
            k = (i * group + g) * per_leaf + b
            p = place_ref[target_ref[k]]
            term = lax.dot_general(half, blk_ref[g * per_leaf + b], NT, preferred_element_type=F32)
            sums_ref[p] += term


def backward_kernel(group, per_leaf, target_ref, place_ref, r_ref, sent_ref, fwd_ref, inv_ref, blk_ref, out_ref):
    i = pl.program_id(0)
    for g in range(group):
        corr = None
        for b in range(per_leaf):
            k = (i * group + g) * per_leaf + b
            p = place_ref[target_ref[k]]
            term = lax.dot_general(sent_ref[p], blk_ref[g * per_leaf + b], NN, preferred_element_type=F32)
            corr = term if corr is None else corr + term
        back = (fwd_ref[g] - corr).astype(BF16)
        out_ref[g] = lax.dot_general(back, inv_ref[g], NN, preferred_element_type=F32)


def shift_pairs(size, shift):
    return [(i, (i + shift) % size) for i in range(size)]


def on_device(
    leaf_right, upper_right, leaf_inverse, upper_inverse, update_blocks, block_target, upper_place
):
    leaf_count, columns, width = leaf_right.shape
    block_count = update_blocks.shape[0]
    per_leaf = block_count // leaf_count
    upper_total = upper_place.shape[0]
    upper_rows = upper_right.shape[0]
    piece = leaf_inverse.shape[0]
    rhs_size = leaf_count // piece
    leaf_size = upper_total // upper_rows
    group = _group(piece)
    steps = leaf_count // group
    r = lax.axis_index("rhs")
    l = lax.axis_index("leaf")

    inv_pieces = [leaf_inverse] + [
        lax.ppermute(leaf_inverse, "rhs", shift_pairs(rhs_size, s)) for s in range(1, rhs_size)
    ]
    inv_stacked = jnp.concatenate(inv_pieces, axis=0)

    target = block_target.reshape(block_count)
    place = upper_place.astype(jnp.int32)
    rr = jnp.reshape(r, (1,)).astype(jnp.int32)
    params = pltpu.CompilerParams(
        dimension_semantics=("arbitrary",), vmem_limit_bytes=48 * 1024 * 1024
    )

    def inv_map(i, t, q, rv):
        j = (i * group) // piece
        row = ((rv[0] - j + rhs_size) % rhs_size) * piece + (i * group) % piece
        return (row // group, 0, 0)

    fwd_flops = 2 * leaf_count * columns * width * width * (1 + per_leaf)
    cost = pl.CostEstimate(
        flops=fwd_flops,
        transcendentals=0,
        bytes_accessed=update_blocks.size * 2 + leaf_right.size * 8 + inv_stacked.size * 2,
    )
    leaf_forward, sums = pl.pallas_call(
        functools.partial(forward_kernel, group, per_leaf),
        grid_spec=pltpu.PrefetchScalarGridSpec(
            num_scalar_prefetch=3,
            grid=(steps,),
            in_specs=[
                pl.BlockSpec((group, columns, width), lambda i, t, q, rv: (i, 0, 0)),
                pl.BlockSpec((group, width, width), inv_map),
                pl.BlockSpec((group * per_leaf, width, width), lambda i, t, q, rv: (i, 0, 0)),
            ],
            out_specs=[
                pl.BlockSpec((group, columns, width), lambda i, t, q, rv: (i, 0, 0)),
                pl.BlockSpec((upper_total, columns, width), lambda i, t, q, rv: (0, 0, 0)),
            ],
        ),
        out_shape=[
            jax.ShapeDtypeStruct((leaf_count, columns, width), F32),
            jax.ShapeDtypeStruct((upper_total, columns, width), F32),
        ],
        compiler_params=params,
        cost_estimate=cost,
    )(target, place, rr, leaf_right, inv_stacked, update_blocks)

    own = lax.dynamic_slice_in_dim(sums, l * upper_rows, upper_rows, 0)
    for s in range(1, leaf_size):
        dest = (l + s) % leaf_size
        chunk = lax.dynamic_slice_in_dim(sums, dest * upper_rows, upper_rows, 0)
        own = own + lax.ppermute(chunk, "leaf", shift_pairs(leaf_size, s))
    upper_rounded = (upper_right - own).astype(BF16)
    upper_half = jnp.einsum(
        "pcw,pvw->pcv", upper_rounded, upper_inverse, preferred_element_type=F32
    ).astype(BF16)
    upper_solution = jnp.einsum(
        "pcw,pwv->pcv", upper_half, upper_inverse, preferred_element_type=F32
    )
    sent = upper_solution.astype(BF16)
    sent_stacked = jnp.concatenate(
        [sent] + [lax.ppermute(sent, "leaf", shift_pairs(leaf_size, s)) for s in range(1, leaf_size)],
        axis=0,
    )
    owner = place // upper_rows
    place_stacked = ((l - owner + leaf_size) % leaf_size) * upper_rows + place % upper_rows

    leaf_solution = pl.pallas_call(
        functools.partial(backward_kernel, group, per_leaf),
        grid_spec=pltpu.PrefetchScalarGridSpec(
            num_scalar_prefetch=3,
            grid=(steps,),
            in_specs=[
                pl.BlockSpec((upper_total, columns, width), lambda i, t, q, rv: (0, 0, 0)),
                pl.BlockSpec((group, columns, width), lambda i, t, q, rv: (i, 0, 0)),
                pl.BlockSpec((group, width, width), inv_map),
                pl.BlockSpec((group * per_leaf, width, width), lambda i, t, q, rv: (i, 0, 0)),
            ],
            out_specs=pl.BlockSpec((group, columns, width), lambda i, t, q, rv: (i, 0, 0)),
        ),
        out_shape=jax.ShapeDtypeStruct((leaf_count, columns, width), F32),
        compiler_params=params,
        cost_estimate=cost,
    )(target, place_stacked.astype(jnp.int32), rr, sent_stacked, leaf_forward, inv_stacked, update_blocks)
    return (leaf_solution, upper_solution)


def solution(mesh):
    return jax.shard_map(
        on_device,
        mesh=mesh,
        in_specs=(
            P("leaf", "rhs", None),
            P("leaf", "rhs", None),
            P(("leaf", "rhs"), None, None),
            P("leaf", None, None),
            P("leaf", None, None),
            P("leaf", None),
            P(),
        ),
        out_specs=(P("leaf", "rhs", None), P("leaf", "rhs", None)),
        check_vma=False,
    )
```

```python
import functools

import jax
import jax.numpy as jnp
from jax import lax
from jax.experimental import pallas as pl
from jax.experimental.pallas import tpu as pltpu
from jax.sharding import PartitionSpec as P

F32 = jnp.float32
BF16 = jnp.bfloat16
NT = (((1,), (1,)), ((), ()))
NN = (((1,), (0,)), ((), ()))


def _group(count):
    for g in (4, 2, 1):
        if count % g == 0:
            return g
    return 1


def forward_kernel(group, per_leaf, target_ref, place_ref, r_ref, right_ref, inv_ref, blk_ref, fwd_ref, sums_ref):
    i = pl.program_id(0)

    @pl.when(i == 0)
    def _():
        sums_ref[...] = jnp.zeros_like(sums_ref)

    for g in range(group):
        rounded = right_ref[g].astype(BF16)
        forward = lax.dot_general(rounded, inv_ref[g], NT, preferred_element_type=F32)
        fwd_ref[g] = forward
        half = forward.astype(BF16)
        for b in range(per_leaf):
            k = (i * group + g) * per_leaf + b
            p = place_ref[target_ref[k]]
            term = lax.dot_general(half, blk_ref[g * per_leaf + b], NT, preferred_element_type=F32)
            sums_ref[p] += term


def backward_kernel(group, per_leaf, target_ref, place_ref, r_ref, sent_ref, fwd_ref, inv_ref, blk_ref, out_ref):
    i = pl.program_id(0)
    for g in range(group):
        corr = None
        for b in range(per_leaf):
            k = (i * group + g) * per_leaf + b
            p = place_ref[target_ref[k]]
            term = lax.dot_general(sent_ref[p], blk_ref[g * per_leaf + b], NN, preferred_element_type=F32)
            corr = term if corr is None else corr + term
        back = (fwd_ref[g] - corr).astype(BF16)
        out_ref[g] = lax.dot_general(back, inv_ref[g], NN, preferred_element_type=F32)


def shift_pairs(size, shift):
    return [(i, (i + shift) % size) for i in range(size)]


def on_device(
    leaf_right, upper_right, leaf_inverse, upper_inverse, update_blocks, block_target, upper_place
):
    leaf_count, columns, width = leaf_right.shape
    block_count = update_blocks.shape[0]
    per_leaf = block_count // leaf_count
    upper_total = upper_place.shape[0]
    upper_rows = upper_right.shape[0]
    piece = leaf_inverse.shape[0]
    rhs_size = leaf_count // piece
    leaf_size = upper_total // upper_rows
    group = _group(piece)
    steps = leaf_count // group
    r = lax.axis_index("rhs")
    l = lax.axis_index("leaf")

    inv_copies = jnp.broadcast_to(leaf_inverse[None], (rhs_size,) + leaf_inverse.shape)
    inv_stacked = lax.all_to_all(inv_copies, "rhs", 0, 0, tiled=False).reshape(
        (leaf_count,) + leaf_inverse.shape[1:]
    )

    target = block_target.reshape(block_count)
    place = upper_place.astype(jnp.int32)
    rr = jnp.reshape(r, (1,)).astype(jnp.int32)
    params = pltpu.CompilerParams(
        dimension_semantics=("arbitrary",), vmem_limit_bytes=48 * 1024 * 1024
    )

    def inv_map(i, t, q, rv):
        return (i, 0, 0)

    fwd_flops = 2 * leaf_count * columns * width * width * (1 + per_leaf)
    cost = pl.CostEstimate(
        flops=fwd_flops,
        transcendentals=0,
        bytes_accessed=update_blocks.size * 2 + leaf_right.size * 8 + inv_stacked.size * 2,
    )
    leaf_forward, sums = pl.pallas_call(
        functools.partial(forward_kernel, group, per_leaf),
        grid_spec=pltpu.PrefetchScalarGridSpec(
            num_scalar_prefetch=3,
            grid=(steps,),
            in_specs=[
                pl.BlockSpec((group, columns, width), lambda i, t, q, rv: (i, 0, 0)),
                pl.BlockSpec((group, width, width), inv_map),
                pl.BlockSpec((group * per_leaf, width, width), lambda i, t, q, rv: (i, 0, 0)),
            ],
            out_specs=[
                pl.BlockSpec((group, columns, width), lambda i, t, q, rv: (i, 0, 0)),
                pl.BlockSpec((upper_total, columns, width), lambda i, t, q, rv: (0, 0, 0)),
            ],
        ),
        out_shape=[
            jax.ShapeDtypeStruct((leaf_count, columns, width), F32),
            jax.ShapeDtypeStruct((upper_total, columns, width), F32),
        ],
        compiler_params=params,
        cost_estimate=cost,
    )(target, place, rr, leaf_right, inv_stacked, update_blocks)

    parts = lax.all_to_all(
        sums.reshape(leaf_size, upper_rows, columns, width), "leaf", 0, 0, tiled=False
    )
    own = jnp.sum(parts, axis=0)
    upper_rounded = (upper_right - own).astype(BF16)
    upper_half = jnp.einsum(
        "pcw,pvw->pcv", upper_rounded, upper_inverse, preferred_element_type=F32
    ).astype(BF16)
    upper_solution = jnp.einsum(
        "pcw,pwv->pcv", upper_half, upper_inverse, preferred_element_type=F32
    )
    sent = upper_solution.astype(BF16)
    sent_copies = jnp.broadcast_to(sent[None], (leaf_size,) + sent.shape)
    sent_all = lax.all_to_all(sent_copies, "leaf", 0, 0, tiled=False).reshape(
        (upper_total, columns, width)
    )

    leaf_solution = pl.pallas_call(
        functools.partial(backward_kernel, group, per_leaf),
        grid_spec=pltpu.PrefetchScalarGridSpec(
            num_scalar_prefetch=3,
            grid=(steps,),
            in_specs=[
                pl.BlockSpec((upper_total, columns, width), lambda i, t, q, rv: (0, 0, 0)),
                pl.BlockSpec((group, columns, width), lambda i, t, q, rv: (i, 0, 0)),
                pl.BlockSpec((group, width, width), inv_map),
                pl.BlockSpec((group * per_leaf, width, width), lambda i, t, q, rv: (i, 0, 0)),
            ],
            out_specs=pl.BlockSpec((group, columns, width), lambda i, t, q, rv: (i, 0, 0)),
        ),
        out_shape=jax.ShapeDtypeStruct((leaf_count, columns, width), F32),
        compiler_params=params,
        cost_estimate=cost,
    )(target, place, rr, sent_all, leaf_forward, inv_stacked, update_blocks)
    return (leaf_solution, upper_solution)


def solution(mesh):
    return jax.shard_map(
        on_device,
        mesh=mesh,
        in_specs=(
            P("leaf", "rhs", None),
            P("leaf", "rhs", None),
            P(("leaf", "rhs"), None, None),
            P("leaf", None, None),
            P("leaf", None, None),
            P("leaf", None),
            P(),
        ),
        out_specs=(P("leaf", "rhs", None), P("leaf", "rhs", None)),
        check_vma=False,
    )
```

```python
import functools

import jax
import jax.numpy as jnp
from jax import lax
from jax.experimental import pallas as pl
from jax.experimental.pallas import tpu as pltpu
from jax.sharding import PartitionSpec as P

F32 = jnp.float32
BF16 = jnp.bfloat16
NT = (((1,), (1,)), ((), ()))
NN = (((1,), (0,)), ((), ()))


def _group(count):
    for g in (4, 2, 1):
        if count % g == 0:
            return g
    return 1


def forward_kernel(group, per_leaf, target_ref, place_ref, r_ref, right_ref, inv_ref, blk_ref, fwd_ref, sums_ref):
    i = pl.program_id(0)

    @pl.when(i == 0)
    def _():
        sums_ref[...] = jnp.zeros_like(sums_ref)

    for g in range(group):
        rounded = right_ref[g].astype(BF16)
        forward = lax.dot_general(rounded, inv_ref[g], NT, preferred_element_type=F32)
        fwd_ref[g] = forward
        half = forward.astype(BF16)
        for b in range(per_leaf):
            k = (i * group + g) * per_leaf + b
            p = place_ref[target_ref[k]]
            term = lax.dot_general(half, blk_ref[g * per_leaf + b], NT, preferred_element_type=F32)
            sums_ref[p] += term


def backward_kernel(group, per_leaf, target_ref, place_ref, r_ref, sent_ref, fwd_ref, inv_ref, blk_ref, out_ref):
    i = pl.program_id(0)
    for g in range(group):
        corr = None
        for b in range(per_leaf):
            k = (i * group + g) * per_leaf + b
            p = place_ref[target_ref[k]]
            term = lax.dot_general(sent_ref[p], blk_ref[g * per_leaf + b], NN, preferred_element_type=F32)
            corr = term if corr is None else corr + term
        back = (fwd_ref[g] - corr).astype(BF16)
        out_ref[g] = lax.dot_general(back, inv_ref[g], NN, preferred_element_type=F32)


def shift_pairs(size, shift):
    return [(i, (i + shift) % size) for i in range(size)]


def on_device(
    leaf_right, upper_right, leaf_inverse, upper_inverse, update_blocks, block_target, upper_place
):
    leaf_count, columns, width = leaf_right.shape
    block_count = update_blocks.shape[0]
    per_leaf = block_count // leaf_count
    upper_total = upper_place.shape[0]
    upper_rows = upper_right.shape[0]
    piece = leaf_inverse.shape[0]
    rhs_size = leaf_count // piece
    leaf_size = upper_total // upper_rows
    group = _group(piece)
    steps = leaf_count // group
    r = lax.axis_index("rhs")
    l = lax.axis_index("leaf")

    hier = rhs_size == 4
    if hier:
        from_x = lax.ppermute(leaf_inverse, "rhs", [(0, 2), (2, 0), (1, 3), (3, 1)])
        swap = [(0, 1), (1, 0), (2, 3), (3, 2)]
        inv_pieces = [leaf_inverse, from_x, lax.ppermute(leaf_inverse, "rhs", swap), lax.ppermute(from_x, "rhs", swap)]
    else:
        inv_pieces = [leaf_inverse] + [
            lax.ppermute(leaf_inverse, "rhs", shift_pairs(rhs_size, s)) for s in range(1, rhs_size)
        ]
    inv_stacked = jnp.concatenate(inv_pieces, axis=0)

    target = block_target.reshape(block_count)
    place = upper_place.astype(jnp.int32)
    rr = jnp.reshape(r, (1,)).astype(jnp.int32)
    params = pltpu.CompilerParams(
        dimension_semantics=("arbitrary",), vmem_limit_bytes=48 * 1024 * 1024
    )

    def inv_map(i, t, q, rv):
        j = (i * group) // piece
        me = rv[0]
        if hier:
            slot = ((me % 2 + j % 2) % 2) * 2 + (me // 2 + j // 2) % 2
        else:
            slot = (me - j + rhs_size) % rhs_size
        return ((slot * piece + (i * group) % piece) // group, 0, 0)

    fwd_flops = 2 * leaf_count * columns * width * width * (1 + per_leaf)
    cost = pl.CostEstimate(
        flops=fwd_flops,
        transcendentals=0,
        bytes_accessed=update_blocks.size * 2 + leaf_right.size * 8 + inv_stacked.size * 2,
    )
    leaf_forward, sums = pl.pallas_call(
        functools.partial(forward_kernel, group, per_leaf),
        grid_spec=pltpu.PrefetchScalarGridSpec(
            num_scalar_prefetch=3,
            grid=(steps,),
            in_specs=[
                pl.BlockSpec((group, columns, width), lambda i, t, q, rv: (i, 0, 0)),
                pl.BlockSpec((group, width, width), inv_map),
                pl.BlockSpec((group * per_leaf, width, width), lambda i, t, q, rv: (i, 0, 0)),
            ],
            out_specs=[
                pl.BlockSpec((group, columns, width), lambda i, t, q, rv: (i, 0, 0)),
                pl.BlockSpec((upper_total, columns, width), lambda i, t, q, rv: (0, 0, 0)),
            ],
        ),
        out_shape=[
            jax.ShapeDtypeStruct((leaf_count, columns, width), F32),
            jax.ShapeDtypeStruct((upper_total, columns, width), F32),
        ],
        compiler_params=params,
        cost_estimate=cost,
    )(target, place, rr, leaf_right, inv_stacked, update_blocks)

    parts = lax.all_to_all(
        sums.astype(BF16).reshape(leaf_size, upper_rows, columns, width), "leaf", 0, 0, tiled=False
    )
    own = jnp.sum(parts.astype(F32), axis=0)
    upper_rounded = (upper_right - own).astype(BF16)
    upper_half = jnp.einsum(
        "pcw,pvw->pcv", upper_rounded, upper_inverse, preferred_element_type=F32
    ).astype(BF16)
    upper_solution = jnp.einsum(
        "pcw,pwv->pcv", upper_half, upper_inverse, preferred_element_type=F32
    )
    sent = upper_solution.astype(BF16)
    sent_copies = jnp.broadcast_to(sent[None], (leaf_size,) + sent.shape)
    sent_all = lax.all_to_all(sent_copies, "leaf", 0, 0, tiled=False).reshape(
        (upper_total, columns, width)
    )

    leaf_solution = pl.pallas_call(
        functools.partial(backward_kernel, group, per_leaf),
        grid_spec=pltpu.PrefetchScalarGridSpec(
            num_scalar_prefetch=3,
            grid=(steps,),
            in_specs=[
                pl.BlockSpec((upper_total, columns, width), lambda i, t, q, rv: (0, 0, 0)),
                pl.BlockSpec((group, columns, width), lambda i, t, q, rv: (i, 0, 0)),
                pl.BlockSpec((group, width, width), inv_map),
                pl.BlockSpec((group * per_leaf, width, width), lambda i, t, q, rv: (i, 0, 0)),
            ],
            out_specs=pl.BlockSpec((group, columns, width), lambda i, t, q, rv: (i, 0, 0)),
        ),
        out_shape=jax.ShapeDtypeStruct((leaf_count, columns, width), F32),
        compiler_params=params,
        cost_estimate=cost,
    )(target, place, rr, sent_all, leaf_forward, inv_stacked, update_blocks)
    return (leaf_solution, upper_solution)


def solution(mesh):
    return jax.shard_map(
        on_device,
        mesh=mesh,
        in_specs=(
            P("leaf", "rhs", None),
            P("leaf", "rhs", None),
            P(("leaf", "rhs"), None, None),
            P("leaf", None, None),
            P("leaf", None, None),
            P("leaf", None),
            P(),
        ),
        out_specs=(P("leaf", "rhs", None), P("leaf", "rhs", None)),
        check_vma=False,
    )
```

```python
import functools

import jax
import jax.numpy as jnp
from jax import lax
from jax.experimental import pallas as pl
from jax.experimental.pallas import tpu as pltpu
from jax.sharding import PartitionSpec as P

F32 = jnp.float32
BF16 = jnp.bfloat16
NT = (((1,), (1,)), ((), ()))
NN = (((1,), (0,)), ((), ()))


def _group(count):
    for g in (4, 2, 1):
        if count % g == 0:
            return g
    return 1


def forward_kernel(group, per_leaf, target_ref, place_ref, r_ref, right_ref, inv_ref, blk_ref, fwd_ref, sums_ref, acc_ref):
    i = pl.program_id(0)
    columns, width = right_ref.shape[1], right_ref.shape[2]
    padded = acc_ref.shape[2]

    @pl.when(i == 0)
    def _():
        acc_ref[...] = jnp.zeros_like(acc_ref)

    for g in range(group):
        rounded = right_ref[g].astype(BF16)
        forward = lax.dot_general(rounded, inv_ref[g], NT, preferred_element_type=F32)
        fwd_ref[g] = forward
        half = forward.astype(BF16)
        if padded > columns:
            half = jnp.concatenate([half, jnp.zeros((padded - columns, width), BF16)], axis=0)
        blocks = blk_ref[g * per_leaf:(g + 1) * per_leaf].reshape(per_leaf * width, width)
        terms = lax.dot_general(blocks, half, NT, preferred_element_type=F32)
        for b in range(per_leaf):
            k = (i * group + g) * per_leaf + b
            p = place_ref[target_ref[k]]
            acc_ref[p] += terms[b * width:(b + 1) * width]

    @pl.when(i == pl.num_programs(0) - 1)
    def _():
        def body(p, carry):
            sums_ref[p] = acc_ref[p].T[:columns]
            return carry

        lax.fori_loop(0, acc_ref.shape[0], body, 0)


def backward_kernel(group, per_leaf, target_ref, place_ref, r_ref, sent_ref, fwd_ref, inv_ref, blk_ref, out_ref):
    i = pl.program_id(0)
    for g in range(group):
        corr = None
        for b in range(per_leaf):
            k = (i * group + g) * per_leaf + b
            p = place_ref[target_ref[k]]
            term = lax.dot_general(sent_ref[p], blk_ref[g * per_leaf + b], NN, preferred_element_type=F32)
            corr = term if corr is None else corr + term
        back = (fwd_ref[g] - corr).astype(BF16)
        out_ref[g] = lax.dot_general(back, inv_ref[g], NN, preferred_element_type=F32)


def shift_pairs(size, shift):
    return [(i, (i + shift) % size) for i in range(size)]


def on_device(
    leaf_right, upper_right, leaf_inverse, upper_inverse, update_blocks, block_target, upper_place
):
    leaf_count, columns, width = leaf_right.shape
    block_count = update_blocks.shape[0]
    per_leaf = block_count // leaf_count
    upper_total = upper_place.shape[0]
    upper_rows = upper_right.shape[0]
    piece = leaf_inverse.shape[0]
    rhs_size = leaf_count // piece
    leaf_size = upper_total // upper_rows
    group = _group(piece)
    steps = leaf_count // group
    r = lax.axis_index("rhs")
    l = lax.axis_index("leaf")

    hier = rhs_size == 4
    if hier:
        from_x = lax.ppermute(leaf_inverse, "rhs", [(0, 2), (2, 0), (1, 3), (3, 1)])
        swap = [(0, 1), (1, 0), (2, 3), (3, 2)]
        inv_pieces = [leaf_inverse, from_x, lax.ppermute(leaf_inverse, "rhs", swap), lax.ppermute(from_x, "rhs", swap)]
    else:
        inv_pieces = [leaf_inverse] + [
            lax.ppermute(leaf_inverse, "rhs", shift_pairs(rhs_size, s)) for s in range(1, rhs_size)
        ]
    inv_stacked = jnp.concatenate(inv_pieces, axis=0)

    target = block_target.reshape(block_count)
    place = upper_place.astype(jnp.int32)
    rr = jnp.reshape(r, (1,)).astype(jnp.int32)
    params = pltpu.CompilerParams(
        dimension_semantics=("arbitrary",), vmem_limit_bytes=48 * 1024 * 1024
    )

    def inv_map(i, t, q, rv):
        j = (i * group) // piece
        me = rv[0]
        if hier:
            slot = ((me % 2 + j % 2) % 2) * 2 + (me // 2 + j // 2) % 2
        else:
            slot = (me - j + rhs_size) % rhs_size
        return ((slot * piece + (i * group) % piece) // group, 0, 0)

    fwd_flops = 2 * leaf_count * columns * width * width * (1 + per_leaf)
    cost = pl.CostEstimate(
        flops=fwd_flops,
        transcendentals=0,
        bytes_accessed=update_blocks.size * 2 + leaf_right.size * 8 + inv_stacked.size * 2,
    )
    leaf_forward, sums = pl.pallas_call(
        functools.partial(forward_kernel, group, per_leaf),
        grid_spec=pltpu.PrefetchScalarGridSpec(
            num_scalar_prefetch=3,
            grid=(steps,),
            in_specs=[
                pl.BlockSpec((group, columns, width), lambda i, t, q, rv: (i, 0, 0)),
                pl.BlockSpec((group, width, width), inv_map),
                pl.BlockSpec((group * per_leaf, width, width), lambda i, t, q, rv: (i, 0, 0)),
            ],
            out_specs=[
                pl.BlockSpec((group, columns, width), lambda i, t, q, rv: (i, 0, 0)),
                pl.BlockSpec((upper_total, columns, width), lambda i, t, q, rv: (0, 0, 0)),
            ],
            scratch_shapes=[pltpu.VMEM((upper_total, width, -(-columns // 128) * 128), F32)],
        ),
        out_shape=[
            jax.ShapeDtypeStruct((leaf_count, columns, width), F32),
            jax.ShapeDtypeStruct((upper_total, columns, width), F32),
        ],
        compiler_params=params,
        cost_estimate=cost,
    )(target, place, rr, leaf_right, inv_stacked, update_blocks)

    if leaf_size % 2 == 0:
        half_size = leaf_size // 2
        y = l % 2
        m = l // 2
        by_parity = sums.reshape(half_size, 2, upper_rows, columns, width)
        mine = lax.dynamic_index_in_dim(by_parity, y, axis=1, keepdims=False)
        theirs = lax.dynamic_index_in_dim(by_parity, 1 - y, axis=1, keepdims=False)
        pairs = [(i, i ^ 1) for i in range(leaf_size)]
        acc = mine + lax.ppermute(theirs, "leaf", pairs)
        own = lax.dynamic_index_in_dim(acc, m, axis=0, keepdims=False)
        for s_ in range(1, half_size):
            chunk = lax.dynamic_index_in_dim(acc, (m + s_) % half_size, axis=0, keepdims=False)
            own = own + lax.ppermute(chunk, "leaf", shift_pairs(leaf_size, 2 * s_))
    else:
        own = lax.dynamic_slice_in_dim(sums, l * upper_rows, upper_rows, 0)
        for s_ in range(1, leaf_size):
            dest = (l + s_) % leaf_size
            chunk = lax.dynamic_slice_in_dim(sums, dest * upper_rows, upper_rows, 0)
            own = own + lax.ppermute(chunk, "leaf", shift_pairs(leaf_size, s_))
    upper_rounded = (upper_right - own).astype(BF16)
    upper_half = jnp.einsum(
        "pcw,pvw->pcv", upper_rounded, upper_inverse, preferred_element_type=F32
    ).astype(BF16)
    upper_solution = jnp.einsum(
        "pcw,pwv->pcv", upper_half, upper_inverse, preferred_element_type=F32
    )
    sent = upper_solution.astype(BF16)
    sent_copies = jnp.broadcast_to(sent[None], (leaf_size,) + sent.shape)
    sent_all = lax.all_to_all(sent_copies, "leaf", 0, 0, tiled=False).reshape(
        (upper_total, columns, width)
    )

    leaf_solution = pl.pallas_call(
        functools.partial(backward_kernel, group, per_leaf),
        grid_spec=pltpu.PrefetchScalarGridSpec(
            num_scalar_prefetch=3,
            grid=(steps,),
            in_specs=[
                pl.BlockSpec((upper_total, columns, width), lambda i, t, q, rv: (0, 0, 0)),
                pl.BlockSpec((group, columns, width), lambda i, t, q, rv: (i, 0, 0)),
                pl.BlockSpec((group, width, width), inv_map),
                pl.BlockSpec((group * per_leaf, width, width), lambda i, t, q, rv: (i, 0, 0)),
            ],
            out_specs=pl.BlockSpec((group, columns, width), lambda i, t, q, rv: (i, 0, 0)),
        ),
        out_shape=jax.ShapeDtypeStruct((leaf_count, columns, width), F32),
        compiler_params=params,
        cost_estimate=cost,
    )(target, place, rr, sent_all, leaf_forward, inv_stacked, update_blocks)
    return (leaf_solution, upper_solution)


def solution(mesh):
    return jax.shard_map(
        on_device,
        mesh=mesh,
        in_specs=(
            P("leaf", "rhs", None),
            P("leaf", "rhs", None),
            P(("leaf", "rhs"), None, None),
            P("leaf", None, None),
            P("leaf", None, None),
            P("leaf", None),
            P(),
        ),
        out_specs=(P("leaf", "rhs", None), P("leaf", "rhs", None)),
        check_vma=False,
    )
```

```python
import functools

import jax
import jax.numpy as jnp
from jax import lax
from jax.experimental import pallas as pl
from jax.experimental.pallas import tpu as pltpu
from jax.sharding import PartitionSpec as P

F32 = jnp.float32
BF16 = jnp.bfloat16
NT = (((1,), (1,)), ((), ()))
NN = (((1,), (0,)), ((), ()))
TN = (((0,), (1,)), ((), ()))


def _group(count):
    for g in (4, 2, 1):
        if count % g == 0:
            return g
    return 1


def forward_kernel(group, per_leaf, target_ref, place_ref, r_ref, right_ref, inv_ref, blk_ref, fwd_ref, sums_ref, acc_ref):
    i = pl.program_id(0)
    columns, width = right_ref.shape[1], right_ref.shape[2]
    padded = acc_ref.shape[2]

    @pl.when(i == 0)
    def _():
        acc_ref[...] = jnp.zeros_like(acc_ref)

    for g in range(group):
        rounded = right_ref[g].astype(BF16)
        forward = lax.dot_general(rounded, inv_ref[g], NT, preferred_element_type=F32)
        fwd_ref[g] = forward
        half = forward.astype(BF16)
        for b in range(per_leaf):
            k = (i * group + g) * per_leaf + b
            p = place_ref[target_ref[k]]
            term = lax.dot_general(blk_ref[g * per_leaf + b], half, NT, preferred_element_type=F32)
            acc_ref[p, :, :columns] += term

    @pl.when(i == pl.num_programs(0) - 1)
    def _():
        def body(p, carry):
            sums_ref[p] = acc_ref[p].T[:columns]
            return carry

        lax.fori_loop(0, acc_ref.shape[0], body, 0)


def backward_kernel(group, per_leaf, target_ref, place_ref, r_ref, sent_ref, fwd_ref, inv_ref, blk_ref, out_ref):
    i = pl.program_id(0)
    for g in range(group):
        corr = None
        for b in range(per_leaf):
            k = (i * group + g) * per_leaf + b
            p = place_ref[target_ref[k]]
            term = lax.dot_general(blk_ref[g * per_leaf + b], sent_ref[p], TN, preferred_element_type=F32)
            corr = term if corr is None else corr + term
        back = (fwd_ref[g] - corr.T).astype(BF16)
        out_ref[g] = lax.dot_general(back, inv_ref[g], NN, preferred_element_type=F32)


def shift_pairs(size, shift):
    return [(i, (i + shift) % size) for i in range(size)]


def on_device(
    leaf_right, upper_right, leaf_inverse, upper_inverse, update_blocks, block_target, upper_place
):
    leaf_count, columns, width = leaf_right.shape
    block_count = update_blocks.shape[0]
    per_leaf = block_count // leaf_count
    upper_total = upper_place.shape[0]
    upper_rows = upper_right.shape[0]
    piece = leaf_inverse.shape[0]
    rhs_size = leaf_count // piece
    leaf_size = upper_total // upper_rows
    group = _group(piece)
    steps = leaf_count // group
    r = lax.axis_index("rhs")
    l = lax.axis_index("leaf")

    hier = rhs_size == 4
    if hier:
        from_x = lax.ppermute(leaf_inverse, "rhs", [(0, 2), (2, 0), (1, 3), (3, 1)])
        swap = [(0, 1), (1, 0), (2, 3), (3, 2)]
        inv_pieces = [leaf_inverse, from_x, lax.ppermute(leaf_inverse, "rhs", swap), lax.ppermute(from_x, "rhs", swap)]
    else:
        inv_pieces = [leaf_inverse] + [
            lax.ppermute(leaf_inverse, "rhs", shift_pairs(rhs_size, s)) for s in range(1, rhs_size)
        ]
    inv_stacked = jnp.concatenate(inv_pieces, axis=0)

    target = block_target.reshape(block_count)
    place = upper_place.astype(jnp.int32)
    rr = jnp.reshape(r, (1,)).astype(jnp.int32)
    params = pltpu.CompilerParams(
        dimension_semantics=("arbitrary",), vmem_limit_bytes=48 * 1024 * 1024
    )

    def inv_map(i, t, q, rv):
        j = (i * group) // piece
        me = rv[0]
        if hier:
            slot = ((me % 2 + j % 2) % 2) * 2 + (me // 2 + j // 2) % 2
        else:
            slot = (me - j + rhs_size) % rhs_size
        return ((slot * piece + (i * group) % piece) // group, 0, 0)

    fwd_flops = 2 * leaf_count * columns * width * width * (1 + per_leaf)
    cost = pl.CostEstimate(
        flops=fwd_flops,
        transcendentals=0,
        bytes_accessed=update_blocks.size * 2 + leaf_right.size * 8 + inv_stacked.size * 2,
    )
    leaf_forward, sums = pl.pallas_call(
        functools.partial(forward_kernel, group, per_leaf),
        grid_spec=pltpu.PrefetchScalarGridSpec(
            num_scalar_prefetch=3,
            grid=(steps,),
            in_specs=[
                pl.BlockSpec((group, columns, width), lambda i, t, q, rv: (i, 0, 0)),
                pl.BlockSpec((group, width, width), inv_map),
                pl.BlockSpec((group * per_leaf, width, width), lambda i, t, q, rv: (i, 0, 0)),
            ],
            out_specs=[
                pl.BlockSpec((group, columns, width), lambda i, t, q, rv: (i, 0, 0)),
                pl.BlockSpec((upper_total, columns, width), lambda i, t, q, rv: (0, 0, 0)),
            ],
            scratch_shapes=[pltpu.VMEM((upper_total, width, -(-columns // 128) * 128), F32)],
        ),
        out_shape=[
            jax.ShapeDtypeStruct((leaf_count, columns, width), F32),
            jax.ShapeDtypeStruct((upper_total, columns, width), F32),
        ],
        compiler_params=params,
        cost_estimate=cost,
    )(target, place, rr, leaf_right, inv_stacked, update_blocks)

    if leaf_size % 2 == 0:
        half_size = leaf_size // 2
        y = l % 2
        m = l // 2
        by_parity = sums.reshape(half_size, 2, upper_rows, columns, width)
        mine = lax.dynamic_index_in_dim(by_parity, y, axis=1, keepdims=False)
        theirs = lax.dynamic_index_in_dim(by_parity, 1 - y, axis=1, keepdims=False)
        pairs = [(i, i ^ 1) for i in range(leaf_size)]
        acc = mine + lax.ppermute(theirs, "leaf", pairs)
        own = lax.dynamic_index_in_dim(acc, m, axis=0, keepdims=False)
        for s_ in range(1, half_size):
            chunk = lax.dynamic_index_in_dim(acc, (m + s_) % half_size, axis=0, keepdims=False)
            own = own + lax.ppermute(chunk, "leaf", shift_pairs(leaf_size, 2 * s_))
    else:
        own = lax.dynamic_slice_in_dim(sums, l * upper_rows, upper_rows, 0)
        for s_ in range(1, leaf_size):
            dest = (l + s_) % leaf_size
            chunk = lax.dynamic_slice_in_dim(sums, dest * upper_rows, upper_rows, 0)
            own = own + lax.ppermute(chunk, "leaf", shift_pairs(leaf_size, s_))
    upper_rounded = (upper_right - own).astype(BF16)
    upper_half = jnp.einsum(
        "pcw,pvw->pcv", upper_rounded, upper_inverse, preferred_element_type=F32
    ).astype(BF16)
    upper_solution = jnp.einsum(
        "pcw,pwv->pcv", upper_half, upper_inverse, preferred_element_type=F32
    )
    sent = upper_solution.astype(BF16)
    sent_copies = jnp.broadcast_to(sent[None], (leaf_size,) + sent.shape)
    sent_all = lax.all_to_all(sent_copies, "leaf", 0, 0, tiled=False).reshape(
        (upper_total, columns, width)
    )

    leaf_solution = pl.pallas_call(
        functools.partial(backward_kernel, group, per_leaf),
        grid_spec=pltpu.PrefetchScalarGridSpec(
            num_scalar_prefetch=3,
            grid=(steps,),
            in_specs=[
                pl.BlockSpec((upper_total, columns, width), lambda i, t, q, rv: (0, 0, 0)),
                pl.BlockSpec((group, columns, width), lambda i, t, q, rv: (i, 0, 0)),
                pl.BlockSpec((group, width, width), inv_map),
                pl.BlockSpec((group * per_leaf, width, width), lambda i, t, q, rv: (i, 0, 0)),
            ],
            out_specs=pl.BlockSpec((group, columns, width), lambda i, t, q, rv: (i, 0, 0)),
        ),
        out_shape=jax.ShapeDtypeStruct((leaf_count, columns, width), F32),
        compiler_params=params,
        cost_estimate=cost,
    )(target, place, rr, sent_all, leaf_forward, inv_stacked, update_blocks)
    return (leaf_solution, upper_solution)


def solution(mesh):
    return jax.shard_map(
        on_device,
        mesh=mesh,
        in_specs=(
            P("leaf", "rhs", None),
            P("leaf", "rhs", None),
            P(("leaf", "rhs"), None, None),
            P("leaf", None, None),
            P("leaf", None, None),
            P("leaf", None),
            P(),
        ),
        out_specs=(P("leaf", "rhs", None), P("leaf", "rhs", None)),
        check_vma=False,
    )
```

```python
import functools

import jax
import jax.numpy as jnp
from jax import lax
from jax.experimental import pallas as pl
from jax.experimental.pallas import tpu as pltpu
from jax.sharding import PartitionSpec as P

F32 = jnp.float32
BF16 = jnp.bfloat16
NT = (((1,), (1,)), ((), ()))
NN = (((1,), (0,)), ((), ()))


def _group(count):
    for g in (8, 4, 2, 1):
        if count % g == 0:
            return g
    return 1


def forward_kernel(group, per_leaf, target_ref, place_ref, r_ref, right_ref, inv_ref, blk_ref, fwd_ref, sums_ref, acc_ref):
    i = pl.program_id(0)
    columns, width = right_ref.shape[1], right_ref.shape[2]
    padded = acc_ref.shape[2]

    @pl.when(i == 0)
    def _():
        acc_ref[...] = jnp.zeros_like(acc_ref)

    for g in range(group):
        rounded = right_ref[g].astype(BF16)
        forward = lax.dot_general(rounded, inv_ref[g], NT, preferred_element_type=F32)
        fwd_ref[g] = forward
        half = forward.astype(BF16)
        if padded > columns:
            half = jnp.concatenate([half, jnp.zeros((padded - columns, width), BF16)], axis=0)
        blocks = blk_ref[g * per_leaf:(g + 1) * per_leaf].reshape(per_leaf * width, width)
        terms = lax.dot_general(blocks, half, NT, preferred_element_type=F32)
        for b in range(per_leaf):
            k = (i * group + g) * per_leaf + b
            p = place_ref[target_ref[k]]
            acc_ref[p] += terms[b * width:(b + 1) * width]

    @pl.when(i == pl.num_programs(0) - 1)
    def _():
        def body(p, carry):
            sums_ref[p] = acc_ref[p].T[:columns]
            return carry

        lax.fori_loop(0, acc_ref.shape[0], body, 0)


def backward_kernel(group, per_leaf, target_ref, place_ref, r_ref, sent_ref, fwd_ref, inv_ref, blk_ref, out_ref):
    i = pl.program_id(0)
    for g in range(group):
        corr = None
        for b in range(per_leaf):
            k = (i * group + g) * per_leaf + b
            p = place_ref[target_ref[k]]
            term = lax.dot_general(sent_ref[p], blk_ref[g * per_leaf + b], NN, preferred_element_type=F32)
            corr = term if corr is None else corr + term
        back = (fwd_ref[g] - corr).astype(BF16)
        out_ref[g] = lax.dot_general(back, inv_ref[g], NN, preferred_element_type=F32)


def shift_pairs(size, shift):
    return [(i, (i + shift) % size) for i in range(size)]


def on_device(
    leaf_right, upper_right, leaf_inverse, upper_inverse, update_blocks, block_target, upper_place
):
    leaf_count, columns, width = leaf_right.shape
    block_count = update_blocks.shape[0]
    per_leaf = block_count // leaf_count
    upper_total = upper_place.shape[0]
    upper_rows = upper_right.shape[0]
    piece = leaf_inverse.shape[0]
    rhs_size = leaf_count // piece
    leaf_size = upper_total // upper_rows
    group = _group(piece)
    steps = leaf_count // group
    r = lax.axis_index("rhs")
    l = lax.axis_index("leaf")

    hier = rhs_size == 4
    if hier:
        from_x = lax.ppermute(leaf_inverse, "rhs", [(0, 2), (2, 0), (1, 3), (3, 1)])
        swap = [(0, 1), (1, 0), (2, 3), (3, 2)]
        inv_pieces = [leaf_inverse, from_x, lax.ppermute(leaf_inverse, "rhs", swap), lax.ppermute(from_x, "rhs", swap)]
    else:
        inv_pieces = [leaf_inverse] + [
            lax.ppermute(leaf_inverse, "rhs", shift_pairs(rhs_size, s)) for s in range(1, rhs_size)
        ]
    inv_stacked = jnp.concatenate(inv_pieces, axis=0)

    target = block_target.reshape(block_count)
    place = upper_place.astype(jnp.int32)
    rr = jnp.reshape(r, (1,)).astype(jnp.int32)
    params = pltpu.CompilerParams(
        dimension_semantics=("arbitrary",), vmem_limit_bytes=48 * 1024 * 1024
    )

    def inv_map(i, t, q, rv):
        j = (i * group) // piece
        me = rv[0]
        if hier:
            slot = ((me % 2 + j % 2) % 2) * 2 + (me // 2 + j // 2) % 2
        else:
            slot = (me - j + rhs_size) % rhs_size
        return ((slot * piece + (i * group) % piece) // group, 0, 0)

    fwd_flops = 2 * leaf_count * columns * width * width * (1 + per_leaf)
    cost = pl.CostEstimate(
        flops=fwd_flops,
        transcendentals=0,
        bytes_accessed=update_blocks.size * 2 + leaf_right.size * 8 + inv_stacked.size * 2,
    )
    leaf_forward, sums = pl.pallas_call(
        functools.partial(forward_kernel, group, per_leaf),
        grid_spec=pltpu.PrefetchScalarGridSpec(
            num_scalar_prefetch=3,
            grid=(steps,),
            in_specs=[
                pl.BlockSpec((group, columns, width), lambda i, t, q, rv: (i, 0, 0)),
                pl.BlockSpec((group, width, width), inv_map),
                pl.BlockSpec((group * per_leaf, width, width), lambda i, t, q, rv: (i, 0, 0)),
            ],
            out_specs=[
                pl.BlockSpec((group, columns, width), lambda i, t, q, rv: (i, 0, 0)),
                pl.BlockSpec((upper_total, columns, width), lambda i, t, q, rv: (0, 0, 0)),
            ],
            scratch_shapes=[pltpu.VMEM((upper_total, width, -(-columns // 128) * 128), F32)],
        ),
        out_shape=[
            jax.ShapeDtypeStruct((leaf_count, columns, width), F32),
            jax.ShapeDtypeStruct((upper_total, columns, width), F32),
        ],
        compiler_params=params,
        cost_estimate=cost,
    )(target, place, rr, leaf_right, inv_stacked, update_blocks)

    if leaf_size % 2 == 0:
        half_size = leaf_size // 2
        y = l % 2
        m = l // 2
        by_parity = sums.reshape(half_size, 2, upper_rows, columns, width)
        mine = lax.dynamic_index_in_dim(by_parity, y, axis=1, keepdims=False)
        theirs = lax.dynamic_index_in_dim(by_parity, 1 - y, axis=1, keepdims=False)
        pairs = [(i, i ^ 1) for i in range(leaf_size)]
        acc = mine + lax.ppermute(theirs, "leaf", pairs)
        own = lax.dynamic_index_in_dim(acc, m, axis=0, keepdims=False)
        for s_ in range(1, half_size):
            chunk = lax.dynamic_index_in_dim(acc, (m + s_) % half_size, axis=0, keepdims=False)
            own = own + lax.ppermute(chunk, "leaf", shift_pairs(leaf_size, 2 * s_))
    else:
        own = lax.dynamic_slice_in_dim(sums, l * upper_rows, upper_rows, 0)
        for s_ in range(1, leaf_size):
            dest = (l + s_) % leaf_size
            chunk = lax.dynamic_slice_in_dim(sums, dest * upper_rows, upper_rows, 0)
            own = own + lax.ppermute(chunk, "leaf", shift_pairs(leaf_size, s_))
    upper_rounded = (upper_right - own).astype(BF16)
    upper_half = jnp.einsum(
        "pcw,pvw->pcv", upper_rounded, upper_inverse, preferred_element_type=F32
    ).astype(BF16)
    upper_solution = jnp.einsum(
        "pcw,pwv->pcv", upper_half, upper_inverse, preferred_element_type=F32
    )
    sent = upper_solution.astype(BF16)
    sent_copies = jnp.broadcast_to(sent[None], (leaf_size,) + sent.shape)
    sent_all = lax.all_to_all(sent_copies, "leaf", 0, 0, tiled=False).reshape(
        (upper_total, columns, width)
    )

    leaf_solution = pl.pallas_call(
        functools.partial(backward_kernel, group, per_leaf),
        grid_spec=pltpu.PrefetchScalarGridSpec(
            num_scalar_prefetch=3,
            grid=(steps,),
            in_specs=[
                pl.BlockSpec((upper_total, columns, width), lambda i, t, q, rv: (0, 0, 0)),
                pl.BlockSpec((group, columns, width), lambda i, t, q, rv: (i, 0, 0)),
                pl.BlockSpec((group, width, width), inv_map),
                pl.BlockSpec((group * per_leaf, width, width), lambda i, t, q, rv: (i, 0, 0)),
            ],
            out_specs=pl.BlockSpec((group, columns, width), lambda i, t, q, rv: (i, 0, 0)),
        ),
        out_shape=jax.ShapeDtypeStruct((leaf_count, columns, width), F32),
        compiler_params=params,
        cost_estimate=cost,
    )(target, place, rr, sent_all, leaf_forward, inv_stacked, update_blocks)
    return (leaf_solution, upper_solution)


def solution(mesh):
    return jax.shard_map(
        on_device,
        mesh=mesh,
        in_specs=(
            P("leaf", "rhs", None),
            P("leaf", "rhs", None),
            P(("leaf", "rhs"), None, None),
            P("leaf", None, None),
            P("leaf", None, None),
            P("leaf", None),
            P(),
        ),
        out_specs=(P("leaf", "rhs", None), P("leaf", "rhs", None)),
        check_vma=False,
    )
```

```python
import functools

import jax
import jax.numpy as jnp
from jax import lax
from jax.experimental import pallas as pl
from jax.experimental.pallas import tpu as pltpu
from jax.sharding import PartitionSpec as P

F32 = jnp.float32
BF16 = jnp.bfloat16
NT = (((1,), (1,)), ((), ()))
NN = (((1,), (0,)), ((), ()))


def _group(count):
    for g in (16, 8, 4, 2, 1):
        if count % g == 0:
            return g
    return 1


def inv_row(slot_of, piece, r_ref, n):
    return slot_of(r_ref[0], n // piece) * piece + n % piece


def forward_kernel(group, per_leaf, slot_of, piece, target_ref, place_ref, r_ref, right_ref, inv_ref, blk_ref, fwd_ref, sums_ref, acc_ref):
    i = pl.program_id(0)
    columns, width = right_ref.shape[1], right_ref.shape[2]
    padded = acc_ref.shape[2]

    @pl.when(i == 0)
    def _():
        acc_ref[...] = jnp.zeros_like(acc_ref)

    for g in range(group):
        rounded = right_ref[g].astype(BF16)
        inverse = inv_ref[inv_row(slot_of, piece, r_ref, i * group + g)]
        forward = lax.dot_general(rounded, inverse, NT, preferred_element_type=F32)
        fwd_ref[g] = forward
        half = forward.astype(BF16)
        if padded > columns:
            half = jnp.concatenate([half, jnp.zeros((padded - columns, width), BF16)], axis=0)
        blocks = blk_ref[g * per_leaf:(g + 1) * per_leaf].reshape(per_leaf * width, width)
        terms = lax.dot_general(blocks, half, NT, preferred_element_type=F32)
        for b in range(per_leaf):
            k = (i * group + g) * per_leaf + b
            p = place_ref[target_ref[k]]
            acc_ref[p] += terms[b * width:(b + 1) * width]

    @pl.when(i == pl.num_programs(0) - 1)
    def _():
        def body(p, carry):
            sums_ref[p] = acc_ref[p].T[:columns]
            return carry

        lax.fori_loop(0, acc_ref.shape[0], body, 0)


def backward_kernel(group, per_leaf, slot_of, piece, target_ref, place_ref, r_ref, sent_ref, fwd_ref, inv_ref, blk_ref, out_ref):
    i = pl.program_id(0)
    for g in range(group):
        corr = None
        for b in range(per_leaf):
            k = (i * group + g) * per_leaf + b
            p = place_ref[target_ref[k]]
            term = lax.dot_general(sent_ref[p], blk_ref[g * per_leaf + b], NN, preferred_element_type=F32)
            corr = term if corr is None else corr + term
        back = (fwd_ref[g] - corr).astype(BF16)
        inverse = inv_ref[inv_row(slot_of, piece, r_ref, i * group + g)]
        out_ref[g] = lax.dot_general(back, inverse, NN, preferred_element_type=F32)


def shift_pairs(size, shift):
    return [(i, (i + shift) % size) for i in range(size)]


def on_device(
    leaf_right, upper_right, leaf_inverse, upper_inverse, update_blocks, block_target, upper_place
):
    leaf_count, columns, width = leaf_right.shape
    block_count = update_blocks.shape[0]
    per_leaf = block_count // leaf_count
    upper_total = upper_place.shape[0]
    upper_rows = upper_right.shape[0]
    piece = leaf_inverse.shape[0]
    rhs_size = leaf_count // piece
    leaf_size = upper_total // upper_rows
    group = _group(leaf_count)
    steps = leaf_count // group
    r = lax.axis_index("rhs")
    l = lax.axis_index("leaf")

    hier = rhs_size == 4
    if hier:
        from_x = lax.ppermute(leaf_inverse, "rhs", [(0, 2), (2, 0), (1, 3), (3, 1)])
        swap = [(0, 1), (1, 0), (2, 3), (3, 2)]
        inv_pieces = [leaf_inverse, from_x, lax.ppermute(leaf_inverse, "rhs", swap), lax.ppermute(from_x, "rhs", swap)]
    else:
        inv_pieces = [leaf_inverse] + [
            lax.ppermute(leaf_inverse, "rhs", shift_pairs(rhs_size, s)) for s in range(1, rhs_size)
        ]
    inv_stacked = jnp.concatenate(inv_pieces, axis=0)

    target = block_target.reshape(block_count)
    place = upper_place.astype(jnp.int32)
    rr = jnp.reshape(r, (1,)).astype(jnp.int32)
    params = pltpu.CompilerParams(
        dimension_semantics=("arbitrary",), vmem_limit_bytes=60 * 1024 * 1024
    )

    def slot_of(me, j):
        if hier:
            return ((me % 2 + j % 2) % 2) * 2 + (me // 2 + j // 2) % 2
        return (me - j + rhs_size) % rhs_size

    def inv_map(i, t, q, rv):
        return (0, 0, 0)

    fwd_flops = 2 * leaf_count * columns * width * width * (1 + per_leaf)
    cost = pl.CostEstimate(
        flops=fwd_flops,
        transcendentals=0,
        bytes_accessed=update_blocks.size * 2 + leaf_right.size * 8 + inv_stacked.size * 2,
    )
    leaf_forward, sums = pl.pallas_call(
        functools.partial(forward_kernel, group, per_leaf, slot_of, piece),
        grid_spec=pltpu.PrefetchScalarGridSpec(
            num_scalar_prefetch=3,
            grid=(steps,),
            in_specs=[
                pl.BlockSpec((group, columns, width), lambda i, t, q, rv: (i, 0, 0)),
                pl.BlockSpec((leaf_count, width, width), inv_map),
                pl.BlockSpec((group * per_leaf, width, width), lambda i, t, q, rv: (i, 0, 0)),
            ],
            out_specs=[
                pl.BlockSpec((group, columns, width), lambda i, t, q, rv: (i, 0, 0)),
                pl.BlockSpec((upper_total, columns, width), lambda i, t, q, rv: (0, 0, 0)),
            ],
            scratch_shapes=[pltpu.VMEM((upper_total, width, -(-columns // 128) * 128), F32)],
        ),
        out_shape=[
            jax.ShapeDtypeStruct((leaf_count, columns, width), F32),
            jax.ShapeDtypeStruct((upper_total, columns, width), F32),
        ],
        compiler_params=params,
        cost_estimate=cost,
    )(target, place, rr, leaf_right, inv_stacked, update_blocks)

    if leaf_size % 2 == 0:
        half_size = leaf_size // 2
        y = l % 2
        m = l // 2
        by_parity = sums.reshape(half_size, 2, upper_rows, columns, width)
        mine = lax.dynamic_index_in_dim(by_parity, y, axis=1, keepdims=False)
        theirs = lax.dynamic_index_in_dim(by_parity, 1 - y, axis=1, keepdims=False)
        pairs = [(i, i ^ 1) for i in range(leaf_size)]
        acc = mine + lax.ppermute(theirs, "leaf", pairs)
        own = lax.dynamic_index_in_dim(acc, m, axis=0, keepdims=False)
        for s_ in range(1, half_size):
            chunk = lax.dynamic_index_in_dim(acc, (m + s_) % half_size, axis=0, keepdims=False)
            own = own + lax.ppermute(chunk, "leaf", shift_pairs(leaf_size, 2 * s_))
    else:
        own = lax.dynamic_slice_in_dim(sums, l * upper_rows, upper_rows, 0)
        for s_ in range(1, leaf_size):
            dest = (l + s_) % leaf_size
            chunk = lax.dynamic_slice_in_dim(sums, dest * upper_rows, upper_rows, 0)
            own = own + lax.ppermute(chunk, "leaf", shift_pairs(leaf_size, s_))
    upper_rounded = (upper_right - own).astype(BF16)
    upper_half = jnp.einsum(
        "pcw,pvw->pcv", upper_rounded, upper_inverse, preferred_element_type=F32
    ).astype(BF16)
    upper_solution = jnp.einsum(
        "pcw,pwv->pcv", upper_half, upper_inverse, preferred_element_type=F32
    )
    sent = upper_solution.astype(BF16)
    sent_copies = jnp.broadcast_to(sent[None], (leaf_size,) + sent.shape)
    sent_all = lax.all_to_all(sent_copies, "leaf", 0, 0, tiled=False).reshape(
        (upper_total, columns, width)
    )

    leaf_solution = pl.pallas_call(
        functools.partial(backward_kernel, group, per_leaf, slot_of, piece),
        grid_spec=pltpu.PrefetchScalarGridSpec(
            num_scalar_prefetch=3,
            grid=(steps,),
            in_specs=[
                pl.BlockSpec((upper_total, columns, width), lambda i, t, q, rv: (0, 0, 0)),
                pl.BlockSpec((group, columns, width), lambda i, t, q, rv: (i, 0, 0)),
                pl.BlockSpec((leaf_count, width, width), inv_map),
                pl.BlockSpec((group * per_leaf, width, width), lambda i, t, q, rv: (i, 0, 0)),
            ],
            out_specs=pl.BlockSpec((group, columns, width), lambda i, t, q, rv: (i, 0, 0)),
        ),
        out_shape=jax.ShapeDtypeStruct((leaf_count, columns, width), F32),
        compiler_params=params,
        cost_estimate=cost,
    )(target, place, rr, sent_all, leaf_forward, inv_stacked, update_blocks)
    return (leaf_solution, upper_solution)


def solution(mesh):
    return jax.shard_map(
        on_device,
        mesh=mesh,
        in_specs=(
            P("leaf", "rhs", None),
            P("leaf", "rhs", None),
            P(("leaf", "rhs"), None, None),
            P("leaf", None, None),
            P("leaf", None, None),
            P("leaf", None),
            P(),
        ),
        out_specs=(P("leaf", "rhs", None), P("leaf", "rhs", None)),
        check_vma=False,
    )
```

```python
import functools

import jax
import jax.numpy as jnp
from jax import lax
from jax.experimental import pallas as pl
from jax.experimental.pallas import tpu as pltpu
from jax.sharding import PartitionSpec as P

F32 = jnp.float32
BF16 = jnp.bfloat16
NT = (((1,), (1,)), ((), ()))
NN = (((1,), (0,)), ((), ()))


def _group(count):
    for g in (8, 4, 2, 1):
        if count % g == 0:
            return g
    return 1


def forward_kernel(group, per_leaf, pos_ref, r_ref, right_ref, inv_ref, blk_ref, fwd_ref, sums_ref, acc_ref):
    i = pl.program_id(0)
    columns, width = right_ref.shape[1], right_ref.shape[2]
    padded = acc_ref.shape[2]

    @pl.when(i == 0)
    def _():
        acc_ref[...] = jnp.zeros_like(acc_ref)

    for g in range(group):
        rounded = right_ref[g]
        forward = lax.dot_general(rounded, inv_ref[g], NT, preferred_element_type=F32)
        fwd_ref[g] = forward
        half = forward.astype(BF16)
        if padded > columns:
            half = jnp.concatenate([half, jnp.zeros((padded - columns, width), BF16)], axis=0)
        blocks = blk_ref[g * per_leaf:(g + 1) * per_leaf].reshape(per_leaf * width, width)
        terms = lax.dot_general(blocks, half, NT, preferred_element_type=F32)
        for b in range(per_leaf):
            k = (i * group + g) * per_leaf + b
            p = pos_ref[k]
            acc_ref[p] += terms[b * width:(b + 1) * width]

    @pl.when(i == pl.num_programs(0) - 1)
    def _():
        def body(p, carry):
            sums_ref[p] = acc_ref[p].T[:columns]
            return carry

        lax.fori_loop(0, acc_ref.shape[0], body, 0)


def backward_kernel(group, per_leaf, pos_ref, r_ref, sent_ref, fwd_ref, inv_ref, blk_ref, out_ref):
    i = pl.program_id(0)
    for g in range(group):
        corr = None
        for b in range(per_leaf):
            k = (i * group + g) * per_leaf + b
            p = pos_ref[k]
            term = lax.dot_general(sent_ref[p], blk_ref[g * per_leaf + b], NN, preferred_element_type=F32)
            corr = term if corr is None else corr + term
        back = (fwd_ref[g] - corr).astype(BF16)
        out_ref[g] = lax.dot_general(back, inv_ref[g], NN, preferred_element_type=F32)


def shift_pairs(size, shift):
    return [(i, (i + shift) % size) for i in range(size)]


def on_device(
    leaf_right, upper_right, leaf_inverse, upper_inverse, update_blocks, block_target, upper_place
):
    leaf_count, columns, width = leaf_right.shape
    block_count = update_blocks.shape[0]
    per_leaf = block_count // leaf_count
    upper_total = upper_place.shape[0]
    upper_rows = upper_right.shape[0]
    piece = leaf_inverse.shape[0]
    rhs_size = leaf_count // piece
    leaf_size = upper_total // upper_rows
    group = _group(piece)
    steps = leaf_count // group
    r = lax.axis_index("rhs")
    l = lax.axis_index("leaf")

    hier = rhs_size == 4
    if hier:
        from_x = lax.ppermute(leaf_inverse, "rhs", [(0, 2), (2, 0), (1, 3), (3, 1)])
        swap = [(0, 1), (1, 0), (2, 3), (3, 2)]
        inv_pieces = [leaf_inverse, from_x, lax.ppermute(leaf_inverse, "rhs", swap), lax.ppermute(from_x, "rhs", swap)]
    else:
        inv_pieces = [leaf_inverse] + [
            lax.ppermute(leaf_inverse, "rhs", shift_pairs(rhs_size, s)) for s in range(1, rhs_size)
        ]
    inv_stacked = jnp.concatenate(inv_pieces, axis=0)

    position = jnp.take(upper_place.astype(jnp.int32), block_target[:, 0], axis=0)
    leaf_rounded = leaf_right.astype(BF16)
    rr = jnp.reshape(r, (1,)).astype(jnp.int32)
    params = pltpu.CompilerParams(
        dimension_semantics=("arbitrary",), vmem_limit_bytes=48 * 1024 * 1024
    )

    def inv_map(i, t, rv):
        j = (i * group) // piece
        me = rv[0]
        if hier:
            slot = ((me % 2 + j % 2) % 2) * 2 + (me // 2 + j // 2) % 2
        else:
            slot = (me - j + rhs_size) % rhs_size
        return ((slot * piece + (i * group) % piece) // group, 0, 0)

    fwd_flops = 2 * leaf_count * columns * width * width * (1 + per_leaf)
    cost = pl.CostEstimate(
        flops=fwd_flops,
        transcendentals=0,
        bytes_accessed=update_blocks.size * 2 + leaf_right.size * 8 + inv_stacked.size * 2,
    )
    leaf_forward, sums = pl.pallas_call(
        functools.partial(forward_kernel, group, per_leaf),
        grid_spec=pltpu.PrefetchScalarGridSpec(
            num_scalar_prefetch=2,
            grid=(steps,),
            in_specs=[
                pl.BlockSpec((group, columns, width), lambda i, t, rv: (i, 0, 0)),
                pl.BlockSpec((group, width, width), inv_map),
                pl.BlockSpec((group * per_leaf, width, width), lambda i, t, rv: (i, 0, 0)),
            ],
            out_specs=[
                pl.BlockSpec((group, columns, width), lambda i, t, rv: (i, 0, 0)),
                pl.BlockSpec((upper_total, columns, width), lambda i, t, rv: (0, 0, 0)),
            ],
            scratch_shapes=[pltpu.VMEM((upper_total, width, -(-columns // 128) * 128), F32)],
        ),
        out_shape=[
            jax.ShapeDtypeStruct((leaf_count, columns, width), F32),
            jax.ShapeDtypeStruct((upper_total, columns, width), F32),
        ],
        compiler_params=params,
        cost_estimate=cost,
    )(position, rr, leaf_rounded, inv_stacked, update_blocks)

    if leaf_size % 2 == 0:
        half_size = leaf_size // 2
        y = l % 2
        m = l // 2
        by_parity = sums.reshape(half_size, 2, upper_rows, columns, width)
        mine = lax.dynamic_index_in_dim(by_parity, y, axis=1, keepdims=False)
        theirs = lax.dynamic_index_in_dim(by_parity, 1 - y, axis=1, keepdims=False)
        pairs = [(i, i ^ 1) for i in range(leaf_size)]
        acc = mine + lax.ppermute(theirs, "leaf", pairs)
        own = lax.dynamic_index_in_dim(acc, m, axis=0, keepdims=False)
        for s_ in range(1, half_size):
            chunk = lax.dynamic_index_in_dim(acc, (m + s_) % half_size, axis=0, keepdims=False)
            own = own + lax.ppermute(chunk, "leaf", shift_pairs(leaf_size, 2 * s_))
    else:
        own = lax.dynamic_slice_in_dim(sums, l * upper_rows, upper_rows, 0)
        for s_ in range(1, leaf_size):
            dest = (l + s_) % leaf_size
            chunk = lax.dynamic_slice_in_dim(sums, dest * upper_rows, upper_rows, 0)
            own = own + lax.ppermute(chunk, "leaf", shift_pairs(leaf_size, s_))
    upper_rounded = (upper_right - own).astype(BF16)
    upper_half = jnp.einsum(
        "pcw,pvw->pcv", upper_rounded, upper_inverse, preferred_element_type=F32
    ).astype(BF16)
    upper_solution = jnp.einsum(
        "pcw,pwv->pcv", upper_half, upper_inverse, preferred_element_type=F32
    )
    sent = upper_solution.astype(BF16)
    sent_copies = jnp.broadcast_to(sent[None], (leaf_size,) + sent.shape)
    sent_all = lax.all_to_all(sent_copies, "leaf", 0, 0, tiled=False).reshape(
        (upper_total, columns, width)
    )

    leaf_solution = pl.pallas_call(
        functools.partial(backward_kernel, group, per_leaf),
        grid_spec=pltpu.PrefetchScalarGridSpec(
            num_scalar_prefetch=2,
            grid=(steps,),
            in_specs=[
                pl.BlockSpec((upper_total, columns, width), lambda i, t, rv: (0, 0, 0)),
                pl.BlockSpec((group, columns, width), lambda i, t, rv: (i, 0, 0)),
                pl.BlockSpec((group, width, width), inv_map),
                pl.BlockSpec((group * per_leaf, width, width), lambda i, t, rv: (i, 0, 0)),
            ],
            out_specs=pl.BlockSpec((group, columns, width), lambda i, t, rv: (i, 0, 0)),
        ),
        out_shape=jax.ShapeDtypeStruct((leaf_count, columns, width), F32),
        compiler_params=params,
        cost_estimate=cost,
    )(position, rr, sent_all, leaf_forward, inv_stacked, update_blocks)
    return (leaf_solution, upper_solution)


def solution(mesh):
    return jax.shard_map(
        on_device,
        mesh=mesh,
        in_specs=(
            P("leaf", "rhs", None),
            P("leaf", "rhs", None),
            P(("leaf", "rhs"), None, None),
            P("leaf", None, None),
            P("leaf", None, None),
            P("leaf", None),
            P(),
        ),
        out_specs=(P("leaf", "rhs", None), P("leaf", "rhs", None)),
        check_vma=False,
    )
```

```python
import functools

import jax
import jax.numpy as jnp
from jax import lax
from jax.experimental import pallas as pl
from jax.experimental.pallas import tpu as pltpu
from jax.sharding import PartitionSpec as P

F32 = jnp.float32
BF16 = jnp.bfloat16
NT = (((1,), (1,)), ((), ()))
NN = (((1,), (0,)), ((), ()))


def _group(count):
    for g in (16, 8, 4, 2, 1):
        if count % g == 0:
            return g
    return 1


def inv_row(slot_of, piece, r_ref, n):
    return slot_of(r_ref[0], n // piece) * piece + n % piece


def forward_kernel(group, per_leaf, slot_of, piece, target_ref, place_ref, r_ref, right_ref, inv_ref, blk_ref, fwd_ref, sums_ref, acc_ref):
    i = pl.program_id(0)
    columns, width = right_ref.shape[1], right_ref.shape[2]
    padded = acc_ref.shape[2]

    @pl.when(i == 0)
    def _():
        acc_ref[...] = jnp.zeros_like(acc_ref)

    for g in range(group):
        rounded = right_ref[g].astype(BF16)
        inverse = inv_ref[inv_row(slot_of, piece, r_ref, i * group + g)]
        forward = lax.dot_general(rounded, inverse, NT, preferred_element_type=F32)
        fwd_ref[g] = forward
        half = forward.astype(BF16)
        if padded > columns:
            half = jnp.concatenate([half, jnp.zeros((padded - columns, width), BF16)], axis=0)
        blocks = blk_ref[g * per_leaf:(g + 1) * per_leaf].reshape(per_leaf * width, width)
        terms = lax.dot_general(blocks, half, NT, preferred_element_type=F32)
        for b in range(per_leaf):
            k = (i * group + g) * per_leaf + b
            p = place_ref[target_ref[k]]
            acc_ref[p] += terms[b * width:(b + 1) * width]

    @pl.when(i == pl.num_programs(0) - 1)
    def _():
        def body(p, carry):
            sums_ref[p] = acc_ref[p].T[:columns]
            return carry

        lax.fori_loop(0, acc_ref.shape[0], body, 0)


def backward_kernel(group, per_leaf, slot_of, piece, target_ref, place_ref, r_ref, sent_ref, fwd_ref, inv_ref, blk_ref, out_ref):
    i = pl.program_id(0)
    for g in range(group):
        corr = None
        for b in range(per_leaf):
            k = (i * group + g) * per_leaf + b
            p = place_ref[target_ref[k]]
            term = lax.dot_general(sent_ref[p], blk_ref[g * per_leaf + b], NN, preferred_element_type=F32)
            corr = term if corr is None else corr + term
        back = (fwd_ref[g] - corr).astype(BF16)
        inverse = inv_ref[inv_row(slot_of, piece, r_ref, i * group + g)]
        out_ref[g] = lax.dot_general(back, inverse, NN, preferred_element_type=F32)


def shift_pairs(size, shift):
    return [(i, (i + shift) % size) for i in range(size)]


def on_device(
    leaf_right, upper_right, leaf_inverse, upper_inverse, update_blocks, block_target, upper_place
):
    leaf_count, columns, width = leaf_right.shape
    block_count = update_blocks.shape[0]
    per_leaf = block_count // leaf_count
    upper_total = upper_place.shape[0]
    upper_rows = upper_right.shape[0]
    piece = leaf_inverse.shape[0]
    rhs_size = leaf_count // piece
    leaf_size = upper_total // upper_rows
    group = _group(leaf_count)
    steps = leaf_count // group
    r = lax.axis_index("rhs")
    l = lax.axis_index("leaf")

    hier = rhs_size == 4
    if hier:
        from_x = lax.ppermute(leaf_inverse, "rhs", [(0, 2), (2, 0), (1, 3), (3, 1)])
        swap = [(0, 1), (1, 0), (2, 3), (3, 2)]
        inv_pieces = [leaf_inverse, from_x, lax.ppermute(leaf_inverse, "rhs", swap), lax.ppermute(from_x, "rhs", swap)]
    else:
        inv_pieces = [leaf_inverse] + [
            lax.ppermute(leaf_inverse, "rhs", shift_pairs(rhs_size, s)) for s in range(1, rhs_size)
        ]
    inv_stacked = jnp.concatenate(inv_pieces, axis=0)

    target = block_target.reshape(block_count)
    place = upper_place.astype(jnp.int32)
    rr = jnp.reshape(r, (1,)).astype(jnp.int32)
    params = pltpu.CompilerParams(
        dimension_semantics=("arbitrary",), vmem_limit_bytes=48 * 1024 * 1024
    )

    def slot_of(me, j):
        if hier:
            return ((me % 2 + j % 2) % 2) * 2 + (me // 2 + j // 2) % 2
        return (me - j + rhs_size) % rhs_size

    def inv_map(i, t, q, rv):
        return (0, 0, 0)

    fwd_flops = 2 * leaf_count * columns * width * width * (1 + per_leaf)
    cost = pl.CostEstimate(
        flops=fwd_flops,
        transcendentals=0,
        bytes_accessed=update_blocks.size * 2 + leaf_right.size * 8 + inv_stacked.size * 2,
    )
    leaf_forward, sums = pl.pallas_call(
        functools.partial(forward_kernel, group, per_leaf, slot_of, piece),
        grid_spec=pltpu.PrefetchScalarGridSpec(
            num_scalar_prefetch=3,
            grid=(steps,),
            in_specs=[
                pl.BlockSpec((group, columns, width), lambda i, t, q, rv: (i, 0, 0)),
                pl.BlockSpec((leaf_count, width, width), inv_map),
                pl.BlockSpec((group * per_leaf, width, width), lambda i, t, q, rv: (i, 0, 0)),
            ],
            out_specs=[
                pl.BlockSpec((group, columns, width), lambda i, t, q, rv: (i, 0, 0)),
                pl.BlockSpec((upper_total, columns, width), lambda i, t, q, rv: (0, 0, 0)),
            ],
            scratch_shapes=[pltpu.VMEM((upper_total, width, -(-columns // 128) * 128), F32)],
        ),
        out_shape=[
            jax.ShapeDtypeStruct((leaf_count, columns, width), F32),
            jax.ShapeDtypeStruct((upper_total, columns, width), F32),
        ],
        compiler_params=params,
        cost_estimate=cost,
    )(target, place, rr, leaf_right, inv_stacked, update_blocks)

    if leaf_size % 2 == 0:
        half_size = leaf_size // 2
        y = l % 2
        m = l // 2
        by_parity = sums.reshape(half_size, 2, upper_rows, columns, width)
        mine = lax.dynamic_index_in_dim(by_parity, y, axis=1, keepdims=False)
        theirs = lax.dynamic_index_in_dim(by_parity, 1 - y, axis=1, keepdims=False)
        pairs = [(i, i ^ 1) for i in range(leaf_size)]
        acc = mine + lax.ppermute(theirs, "leaf", pairs)
        own = lax.dynamic_index_in_dim(acc, m, axis=0, keepdims=False)
        for s_ in range(1, half_size):
            chunk = lax.dynamic_index_in_dim(acc, (m + s_) % half_size, axis=0, keepdims=False)
            own = own + lax.ppermute(chunk, "leaf", shift_pairs(leaf_size, 2 * s_))
    else:
        own = lax.dynamic_slice_in_dim(sums, l * upper_rows, upper_rows, 0)
        for s_ in range(1, leaf_size):
            dest = (l + s_) % leaf_size
            chunk = lax.dynamic_slice_in_dim(sums, dest * upper_rows, upper_rows, 0)
            own = own + lax.ppermute(chunk, "leaf", shift_pairs(leaf_size, s_))
    upper_rounded = (upper_right - own).astype(BF16)
    upper_half = jnp.einsum(
        "pcw,pvw->pcv", upper_rounded, upper_inverse, preferred_element_type=F32
    ).astype(BF16)
    upper_solution = jnp.einsum(
        "pcw,pwv->pcv", upper_half, upper_inverse, preferred_element_type=F32
    )
    sent = upper_solution.astype(BF16)
    sent_copies = jnp.broadcast_to(sent[None], (leaf_size,) + sent.shape)
    sent_all = lax.all_to_all(sent_copies, "leaf", 0, 0, tiled=False).reshape(
        (upper_total, columns, width)
    )

    leaf_solution = pl.pallas_call(
        functools.partial(backward_kernel, group, per_leaf, slot_of, piece),
        grid_spec=pltpu.PrefetchScalarGridSpec(
            num_scalar_prefetch=3,
            grid=(steps,),
            in_specs=[
                pl.BlockSpec((upper_total, columns, width), lambda i, t, q, rv: (0, 0, 0)),
                pl.BlockSpec((group, columns, width), lambda i, t, q, rv: (i, 0, 0)),
                pl.BlockSpec((leaf_count, width, width), inv_map),
                pl.BlockSpec((group * per_leaf, width, width), lambda i, t, q, rv: (i, 0, 0)),
            ],
            out_specs=pl.BlockSpec((group, columns, width), lambda i, t, q, rv: (i, 0, 0)),
        ),
        out_shape=jax.ShapeDtypeStruct((leaf_count, columns, width), F32),
        compiler_params=params,
        cost_estimate=cost,
    )(target, place, rr, sent_all, leaf_forward, inv_stacked, update_blocks)
    return (leaf_solution, upper_solution)


def solution(mesh):
    return jax.shard_map(
        on_device,
        mesh=mesh,
        in_specs=(
            P("leaf", "rhs", None),
            P("leaf", "rhs", None),
            P(("leaf", "rhs"), None, None),
            P("leaf", None, None),
            P("leaf", None, None),
            P("leaf", None),
            P(),
        ),
        out_specs=(P("leaf", "rhs", None), P("leaf", "rhs", None)),
        check_vma=False,
    )
```

```python
import functools

import jax
import jax.numpy as jnp
from jax import lax
from jax.experimental import pallas as pl
from jax.experimental.pallas import tpu as pltpu
from jax.sharding import PartitionSpec as P

F32 = jnp.float32
BF16 = jnp.bfloat16
NT = (((1,), (1,)), ((), ()))
NN = (((1,), (0,)), ((), ()))


def _group(count):
    for g in (4, 2, 1):
        if count % g == 0:
            return g
    return 1


def forward_kernel(group, per_leaf, piece, first, last, target_ref, place_ref, base_ref, right_ref, inv_ref, blk_ref, *rest):
    if first:
        fwd_ref, acc_ref = rest[0], rest[1]
        outs = rest[2:]
    else:
        acc_in_ref, fwd_ref, acc_ref = rest[0], rest[2], rest[3]
        outs = rest[4:]
    i = pl.program_id(0)
    columns, width = right_ref.shape[1], right_ref.shape[2]
    padded = acc_ref.shape[2]

    @pl.when(i == 0)
    def _():
        if first:
            acc_ref[...] = jnp.zeros_like(acc_ref)
        else:
            acc_ref[...] = acc_in_ref[...]

    for g in range(group):
        rounded = right_ref[g].astype(BF16)
        forward = lax.dot_general(rounded, inv_ref[g], NT, preferred_element_type=F32)
        fwd_ref[g] = forward
        half = forward.astype(BF16)
        if padded > columns:
            half = jnp.concatenate([half, jnp.zeros((padded - columns, width), BF16)], axis=0)
        blocks = blk_ref[g * per_leaf:(g + 1) * per_leaf].reshape(per_leaf * width, width)
        terms = lax.dot_general(blocks, half, NT, preferred_element_type=F32)
        n = base_ref[0] * piece + i * group + g
        for b in range(per_leaf):
            p = place_ref[target_ref[n * per_leaf + b]]
            acc_ref[p] += terms[b * width:(b + 1) * width]

    if last:
        sums_ref = outs[0]

        @pl.when(i == pl.num_programs(0) - 1)
        def _():
            def body(p, carry):
                sums_ref[p] = acc_ref[p].T[:columns]
                return carry

            lax.fori_loop(0, acc_ref.shape[0], body, 0)


def backward_kernel(group, per_leaf, target_ref, place_ref, r_ref, sent_ref, fwd_ref, inv_ref, blk_ref, out_ref):
    i = pl.program_id(0)
    for g in range(group):
        corr = None
        for b in range(per_leaf):
            k = (i * group + g) * per_leaf + b
            p = place_ref[target_ref[k]]
            term = lax.dot_general(sent_ref[p], blk_ref[g * per_leaf + b], NN, preferred_element_type=F32)
            corr = term if corr is None else corr + term
        back = (fwd_ref[g] - corr).astype(BF16)
        out_ref[g] = lax.dot_general(back, inv_ref[g], NN, preferred_element_type=F32)


def shift_pairs(size, shift):
    return [(i, (i + shift) % size) for i in range(size)]


def on_device(
    leaf_right, upper_right, leaf_inverse, upper_inverse, update_blocks, block_target, upper_place
):
    leaf_count, columns, width = leaf_right.shape
    block_count = update_blocks.shape[0]
    per_leaf = block_count // leaf_count
    upper_total = upper_place.shape[0]
    upper_rows = upper_right.shape[0]
    piece = leaf_inverse.shape[0]
    rhs_size = leaf_count // piece
    leaf_size = upper_total // upper_rows
    group = _group(piece)
    bgroup = 8 if piece % 8 == 0 else group
    steps = leaf_count // group
    r = lax.axis_index("rhs")
    l = lax.axis_index("leaf")

    hier = rhs_size == 4
    if hier:
        from_x = lax.ppermute(leaf_inverse, "rhs", [(0, 2), (2, 0), (1, 3), (3, 1)])
        swap = [(0, 1), (1, 0), (2, 3), (3, 2)]
        inv_pieces = [leaf_inverse, from_x, lax.ppermute(leaf_inverse, "rhs", swap), None]
    else:
        inv_pieces = [leaf_inverse] + [
            lax.ppermute(leaf_inverse, "rhs", shift_pairs(rhs_size, s)) for s in range(1, rhs_size)
        ]

    target = block_target.reshape(block_count)
    place = upper_place.astype(jnp.int32)
    rr = jnp.reshape(r, (1,)).astype(jnp.int32)
    params = pltpu.CompilerParams(
        dimension_semantics=("arbitrary",), vmem_limit_bytes=48 * 1024 * 1024
    )

    def inv_map(i, t, q, rv):
        group = bgroup
        j = (i * group) // piece
        me = rv[0]
        if hier:
            slot = ((me % 2 + j % 2) % 2) * 2 + (me // 2 + j // 2) % 2
        else:
            slot = (me - j + rhs_size) % rhs_size
        return ((slot * piece + (i * group) % piece) // group, 0, 0)

    fwd_flops = 2 * leaf_count * columns * width * width * (1 + per_leaf)
    cost = pl.CostEstimate(
        flops=fwd_flops,
        transcendentals=0,
        bytes_accessed=update_blocks.size * 2 + leaf_right.size * 8 + leaf_inverse.size * 2 * rhs_size,
    )
    slot_cost = pl.CostEstimate(
        flops=fwd_flops // rhs_size,
        transcendentals=0,
        bytes_accessed=(update_blocks.size * 2 + leaf_right.size * 8 + leaf_inverse.size * 2 * rhs_size) // rhs_size,
    )
    padded = -(-columns // 128) * 128
    slot_steps = piece // group
    if hier:
        slot_piece = [r, (r + 2) % 4, r + 1 - 2 * (r % 2), 3 - r]
        order = [0, 2, 1, 3]
    else:
        slot_piece = [(r - s_ + rhs_size) % rhs_size for s_ in range(rhs_size)]
        order = list(range(rhs_size))
    acc = None
    leaf_forward = None
    for pos_, s_ in enumerate(order):
        first = pos_ == 0
        last = pos_ == len(order) - 1
        base = jnp.reshape(slot_piece[s_], (1,)).astype(jnp.int32)

        def nat(i, t, q, bv):
            return (bv[0] * slot_steps + i, 0, 0)

        in_specs = [
            pl.BlockSpec((group, columns, width), nat),
            pl.BlockSpec((group, width, width), lambda i, t, q, bv: (i, 0, 0)),
            pl.BlockSpec((group * per_leaf, width, width), nat),
        ]
        if inv_pieces[s_] is None:
            held, _ = lax.optimization_barrier((inv_pieces[1], own_out))
            inv_pieces[s_] = lax.ppermute(held, "rhs", swap)
        operands = [target, place, base, leaf_right, inv_pieces[s_], update_blocks]
        aliases = {}
        if not first:
            in_specs += [
                pl.BlockSpec((upper_total, width, padded), lambda i, t, q, bv: (0, 0, 0)),
                pl.BlockSpec(memory_space=pl.ANY),
            ]
            operands += [acc, leaf_forward]
            aliases = {6: 1, 7: 0}
        out_specs = [
            pl.BlockSpec((group, columns, width), nat),
            pl.BlockSpec((upper_total, width, padded), lambda i, t, q, bv: (0, 0, 0)),
        ]
        out_shape = [
            jax.ShapeDtypeStruct((leaf_count, columns, width), F32),
            jax.ShapeDtypeStruct((upper_total, width, padded), F32),
        ]
        if last:
            out_specs.append(pl.BlockSpec((upper_total, columns, width), lambda i, t, q, bv: (0, 0, 0)))
            out_shape.append(jax.ShapeDtypeStruct((upper_total, columns, width), F32))
        results = pl.pallas_call(
            functools.partial(forward_kernel, group, per_leaf, piece, first, last),
            grid_spec=pltpu.PrefetchScalarGridSpec(
                num_scalar_prefetch=3,
                grid=(slot_steps,),
                in_specs=in_specs,
                out_specs=out_specs,
            ),
            out_shape=out_shape,
            input_output_aliases=aliases,
            compiler_params=params,
            cost_estimate=slot_cost,
        )(*operands)
        leaf_forward, acc = results[0], results[1]
        if first:
            own_out = acc
        if last:
            sums = results[2]

    inv_stacked = jnp.concatenate(inv_pieces, axis=0)
    if leaf_size % 2 == 0:
        half_size = leaf_size // 2
        y = l % 2
        m = l // 2
        by_parity = sums.reshape(half_size, 2, upper_rows, columns, width)
        mine = lax.dynamic_index_in_dim(by_parity, y, axis=1, keepdims=False)
        theirs = lax.dynamic_index_in_dim(by_parity, 1 - y, axis=1, keepdims=False)
        pairs = [(i, i ^ 1) for i in range(leaf_size)]
        acc = mine + lax.ppermute(theirs, "leaf", pairs)
        own = lax.dynamic_index_in_dim(acc, m, axis=0, keepdims=False)
        for s_ in range(1, half_size):
            chunk = lax.dynamic_index_in_dim(acc, (m + s_) % half_size, axis=0, keepdims=False)
            own = own + lax.ppermute(chunk, "leaf", shift_pairs(leaf_size, 2 * s_))
    else:
        own = lax.dynamic_slice_in_dim(sums, l * upper_rows, upper_rows, 0)
        for s_ in range(1, leaf_size):
            dest = (l + s_) % leaf_size
            chunk = lax.dynamic_slice_in_dim(sums, dest * upper_rows, upper_rows, 0)
            own = own + lax.ppermute(chunk, "leaf", shift_pairs(leaf_size, s_))
    upper_rounded = (upper_right - own).astype(BF16)
    upper_half = jnp.einsum(
        "pcw,pvw->pcv", upper_rounded, upper_inverse, preferred_element_type=F32
    ).astype(BF16)
    upper_solution = jnp.einsum(
        "pcw,pwv->pcv", upper_half, upper_inverse, preferred_element_type=F32
    )
    sent = upper_solution.astype(BF16)
    sent_copies = jnp.broadcast_to(sent[None], (leaf_size,) + sent.shape)
    sent_all = lax.all_to_all(sent_copies, "leaf", 0, 0, tiled=False).reshape(
        (upper_total, columns, width)
    )

    leaf_solution = pl.pallas_call(
        functools.partial(backward_kernel, bgroup, per_leaf),
        grid_spec=pltpu.PrefetchScalarGridSpec(
            num_scalar_prefetch=3,
            grid=(leaf_count // bgroup,),
            in_specs=[
                pl.BlockSpec((upper_total, columns, width), lambda i, t, q, rv: (0, 0, 0)),
                pl.BlockSpec((bgroup, columns, width), lambda i, t, q, rv: (i, 0, 0)),
                pl.BlockSpec((bgroup, width, width), inv_map),
                pl.BlockSpec((bgroup * per_leaf, width, width), lambda i, t, q, rv: (i, 0, 0)),
            ],
            out_specs=pl.BlockSpec((bgroup, columns, width), lambda i, t, q, rv: (i, 0, 0)),
        ),
        out_shape=jax.ShapeDtypeStruct((leaf_count, columns, width), F32),
        compiler_params=params,
        cost_estimate=cost,
    )(target, place, rr, sent_all, leaf_forward, inv_stacked, update_blocks)
    return (leaf_solution, upper_solution)


def solution(mesh):
    return jax.shard_map(
        on_device,
        mesh=mesh,
        in_specs=(
            P("leaf", "rhs", None),
            P("leaf", "rhs", None),
            P(("leaf", "rhs"), None, None),
            P("leaf", None, None),
            P("leaf", None, None),
            P("leaf", None),
            P(),
        ),
        out_specs=(P("leaf", "rhs", None), P("leaf", "rhs", None)),
        check_vma=False,
    )
```

```python
import functools

import jax
import jax.numpy as jnp
from jax import lax
from jax.experimental import pallas as pl
from jax.experimental.pallas import tpu as pltpu
from jax.sharding import PartitionSpec as P

F32 = jnp.float32
BF16 = jnp.bfloat16
NT = (((1,), (1,)), ((), ()))
NN = (((1,), (0,)), ((), ()))


def _group(count):
    for g in (8, 4, 2, 1):
        if count % g == 0:
            return g
    return 1


def forward_kernel(per_leaf, piece, first, target_ref, place_ref, base_ref, right_ref, inv_ref, blk_ref, *rest):
    if first:
        fwd_ref, acc_ref = rest
    else:
        acc_in_ref, _, fwd_ref, acc_ref, sums_ref = rest
    i = pl.program_id(0)
    columns, width = right_ref.shape[1], right_ref.shape[2]
    padded = acc_ref.shape[2]

    @pl.when(i == 0)
    def _():
        if first:
            acc_ref[...] = jnp.zeros_like(acc_ref)
        else:
            acc_ref[...] = acc_in_ref[...]

    for g in range(piece):
        rounded = right_ref[g].astype(BF16)
        forward = lax.dot_general(rounded, inv_ref[g], NT, preferred_element_type=F32)
        fwd_ref[g] = forward
        half = forward.astype(BF16)
        if padded > columns:
            half = jnp.concatenate([half, jnp.zeros((padded - columns, width), BF16)], axis=0)
        blocks = blk_ref[g * per_leaf:(g + 1) * per_leaf].reshape(per_leaf * width, width)
        terms = lax.dot_general(blocks, half, NT, preferred_element_type=F32)
        n = base_ref[i] * piece + g
        for b in range(per_leaf):
            p = place_ref[target_ref[n * per_leaf + b]]
            acc_ref[p] += terms[b * width:(b + 1) * width]

    if not first:

        @pl.when(i == pl.num_programs(0) - 1)
        def _():
            def body(p, carry):
                sums_ref[p] = acc_ref[p].T[:columns]
                return carry

            lax.fori_loop(0, acc_ref.shape[0], body, 0)


def backward_kernel(group, per_leaf, target_ref, place_ref, r_ref, sent_ref, fwd_ref, inv_ref, blk_ref, out_ref):
    i = pl.program_id(0)
    for g in range(group):
        corr = None
        for b in range(per_leaf):
            k = (i * group + g) * per_leaf + b
            p = place_ref[target_ref[k]]
            term = lax.dot_general(sent_ref[p], blk_ref[g * per_leaf + b], NN, preferred_element_type=F32)
            corr = term if corr is None else corr + term
        back = (fwd_ref[g] - corr).astype(BF16)
        out_ref[g] = lax.dot_general(back, inv_ref[g], NN, preferred_element_type=F32)


def shift_pairs(size, shift):
    return [(i, (i + shift) % size) for i in range(size)]


def on_device(
    leaf_right, upper_right, leaf_inverse, upper_inverse, update_blocks, block_target, upper_place
):
    leaf_count, columns, width = leaf_right.shape
    block_count = update_blocks.shape[0]
    per_leaf = block_count // leaf_count
    upper_total = upper_place.shape[0]
    upper_rows = upper_right.shape[0]
    piece = leaf_inverse.shape[0]
    rhs_size = leaf_count // piece
    leaf_size = upper_total // upper_rows
    group = _group(piece)
    steps = leaf_count // group
    r = lax.axis_index("rhs")
    l = lax.axis_index("leaf")

    hier = rhs_size == 4
    if hier:
        from_x = lax.ppermute(leaf_inverse, "rhs", [(0, 2), (2, 0), (1, 3), (3, 1)])
        swap = [(0, 1), (1, 0), (2, 3), (3, 2)]
        inv_pieces = [leaf_inverse, from_x, lax.ppermute(leaf_inverse, "rhs", swap), None]
    else:
        inv_pieces = [leaf_inverse] + [
            lax.ppermute(leaf_inverse, "rhs", shift_pairs(rhs_size, s)) for s in range(1, rhs_size)
        ]

    target = block_target.reshape(block_count)
    place = upper_place.astype(jnp.int32)
    rr = jnp.reshape(r, (1,)).astype(jnp.int32)
    params = pltpu.CompilerParams(
        dimension_semantics=("arbitrary",), vmem_limit_bytes=48 * 1024 * 1024
    )

    def inv_map(i, t, q, rv):
        j = (i * group) // piece
        me = rv[0]
        if hier:
            slot = ((me % 2 + j % 2) % 2) * 2 + (me // 2 + j // 2) % 2
        else:
            slot = (me - j + rhs_size) % rhs_size
        return ((slot * piece + (i * group) % piece) // group, 0, 0)

    fwd_flops = 2 * leaf_count * columns * width * width * (1 + per_leaf)
    all_bytes = update_blocks.size * 2 + leaf_right.size * 8 + leaf_inverse.size * 2 * rhs_size
    cost = pl.CostEstimate(flops=fwd_flops, transcendentals=0, bytes_accessed=all_bytes)
    padded = -(-columns // 128) * 128
    if hier:
        slot_piece = [r, (r + 2) % 4, r + 1 - 2 * (r % 2), 3 - r]
        rest_order = [2, 1, 3]
    else:
        slot_piece = [(r - s_ + rhs_size) % rhs_size for s_ in range(rhs_size)]
        rest_order = list(range(1, rhs_size))

    def nat(i, t, q, bv):
        return (bv[i], 0, 0)

    def call(first, bases, inverse, extra):
        count = bases.shape[0]
        in_specs = [
            pl.BlockSpec((piece, columns, width), nat),
            pl.BlockSpec((piece, width, width), lambda i, t, q, bv: (i, 0, 0)),
            pl.BlockSpec((piece * per_leaf, width, width), nat),
        ]
        out_specs = [
            pl.BlockSpec((piece, columns, width), nat),
            pl.BlockSpec((upper_total, width, padded), lambda i, t, q, bv: (0, 0, 0)),
        ]
        out_shape = [
            jax.ShapeDtypeStruct((leaf_count, columns, width), F32),
            jax.ShapeDtypeStruct((upper_total, width, padded), F32),
        ]
        aliases = {}
        if not first:
            in_specs += [
                pl.BlockSpec((upper_total, width, padded), lambda i, t, q, bv: (0, 0, 0)),
                pl.BlockSpec(memory_space=pl.ANY),
            ]
            out_specs.append(pl.BlockSpec((upper_total, columns, width), lambda i, t, q, bv: (0, 0, 0)))
            out_shape.append(jax.ShapeDtypeStruct((upper_total, columns, width), F32))
            aliases = {6: 1, 7: 0}
        return pl.pallas_call(
            functools.partial(forward_kernel, per_leaf, piece, first),
            grid_spec=pltpu.PrefetchScalarGridSpec(
                num_scalar_prefetch=3,
                grid=(count,),
                in_specs=in_specs,
                out_specs=out_specs,
            ),
            out_shape=out_shape,
            input_output_aliases=aliases,
            compiler_params=params,
            cost_estimate=pl.CostEstimate(
                flops=fwd_flops * count // rhs_size,
                transcendentals=0,
                bytes_accessed=all_bytes * count // rhs_size,
            ),
        )(target, place, bases, leaf_right, inverse, update_blocks, *extra)

    own_base = jnp.reshape(slot_piece[0], (1,)).astype(jnp.int32)
    fwd_own, acc_own = call(True, own_base, leaf_inverse, [])
    if hier:
        held, _ = lax.optimization_barrier((from_x, acc_own))
        inv_pieces[3] = lax.ppermute(held, "rhs", swap)
    rest_bases = jnp.stack([slot_piece[s_] for s_ in rest_order]).astype(jnp.int32)
    rest_inv = jnp.concatenate([inv_pieces[s_] for s_ in rest_order], axis=0)
    leaf_forward, _, sums = call(False, rest_bases, rest_inv, [acc_own, fwd_own])
    inv_stacked = jnp.concatenate(inv_pieces, axis=0)

    if leaf_size % 2 == 0:
        half_size = leaf_size // 2
        y = l % 2
        m = l // 2
        by_parity = sums.reshape(half_size, 2, upper_rows, columns, width)
        mine = lax.dynamic_index_in_dim(by_parity, y, axis=1, keepdims=False)
        theirs = lax.dynamic_index_in_dim(by_parity, 1 - y, axis=1, keepdims=False)
        pairs = [(i, i ^ 1) for i in range(leaf_size)]
        acc = mine + lax.ppermute(theirs, "leaf", pairs)
        own = lax.dynamic_index_in_dim(acc, m, axis=0, keepdims=False)
        for s_ in range(1, half_size):
            chunk = lax.dynamic_index_in_dim(acc, (m + s_) % half_size, axis=0, keepdims=False)
            own = own + lax.ppermute(chunk, "leaf", shift_pairs(leaf_size, 2 * s_))
    else:
        own = lax.dynamic_slice_in_dim(sums, l * upper_rows, upper_rows, 0)
        for s_ in range(1, leaf_size):
            dest = (l + s_) % leaf_size
            chunk = lax.dynamic_slice_in_dim(sums, dest * upper_rows, upper_rows, 0)
            own = own + lax.ppermute(chunk, "leaf", shift_pairs(leaf_size, s_))
    upper_rounded = (upper_right - own).astype(BF16)
    upper_half = jnp.einsum(
        "pcw,pvw->pcv", upper_rounded, upper_inverse, preferred_element_type=F32
    ).astype(BF16)
    upper_solution = jnp.einsum(
        "pcw,pwv->pcv", upper_half, upper_inverse, preferred_element_type=F32
    )
    sent = upper_solution.astype(BF16)
    sent_copies = jnp.broadcast_to(sent[None], (leaf_size,) + sent.shape)
    sent_all = lax.all_to_all(sent_copies, "leaf", 0, 0, tiled=False).reshape(
        (upper_total, columns, width)
    )

    leaf_solution = pl.pallas_call(
        functools.partial(backward_kernel, group, per_leaf),
        grid_spec=pltpu.PrefetchScalarGridSpec(
            num_scalar_prefetch=3,
            grid=(steps,),
            in_specs=[
                pl.BlockSpec((upper_total, columns, width), lambda i, t, q, rv: (0, 0, 0)),
                pl.BlockSpec((group, columns, width), lambda i, t, q, rv: (i, 0, 0)),
                pl.BlockSpec((group, width, width), inv_map),
                pl.BlockSpec((group * per_leaf, width, width), lambda i, t, q, rv: (i, 0, 0)),
            ],
            out_specs=pl.BlockSpec((group, columns, width), lambda i, t, q, rv: (i, 0, 0)),
        ),
        out_shape=jax.ShapeDtypeStruct((leaf_count, columns, width), F32),
        compiler_params=params,
        cost_estimate=cost,
    )(target, place, rr, sent_all, leaf_forward, inv_stacked, update_blocks)
    return (leaf_solution, upper_solution)


def solution(mesh):
    return jax.shard_map(
        on_device,
        mesh=mesh,
        in_specs=(
            P("leaf", "rhs", None),
            P("leaf", "rhs", None),
            P(("leaf", "rhs"), None, None),
            P("leaf", None, None),
            P("leaf", None, None),
            P("leaf", None),
            P(),
        ),
        out_specs=(P("leaf", "rhs", None), P("leaf", "rhs", None)),
        check_vma=False,
    )
```

```python
import functools

import jax
import jax.numpy as jnp
from jax import lax
from jax.experimental import pallas as pl
from jax.experimental.pallas import tpu as pltpu
from jax.sharding import PartitionSpec as P

F32 = jnp.float32
BF16 = jnp.bfloat16
NT = (((1,), (1,)), ((), ()))
NN = (((1,), (0,)), ((), ()))


def _group(count):
    for g in (8, 4, 2, 1):
        if count % g == 0:
            return g
    return 1


def forward_kernel(per_leaf, piece, first, count, target_ref, place_ref, base_ref, right_ref, *rest):
    inv_refs = rest[:count]
    blk_ref = rest[count]
    rest = rest[count + 1:]
    if first:
        fwd_ref, acc_ref = rest
    else:
        acc_in_ref, _, fwd_ref, acc_ref, sums_ref = rest
    i = pl.program_id(0)
    columns, width = right_ref.shape[1], right_ref.shape[2]
    padded = acc_ref.shape[2]

    @pl.when(i == 0)
    def _():
        if first:
            acc_ref[...] = jnp.zeros_like(acc_ref)
        else:
            acc_ref[...] = acc_in_ref[...]

    def step(inv_ref):
        for g in range(piece):
            rounded = right_ref[g].astype(BF16)
            forward = lax.dot_general(rounded, inv_ref[g], NT, preferred_element_type=F32)
            fwd_ref[g] = forward
            half = forward.astype(BF16)
            if padded > columns:
                half = jnp.concatenate([half, jnp.zeros((padded - columns, width), BF16)], axis=0)
            blocks = blk_ref[g * per_leaf:(g + 1) * per_leaf].reshape(per_leaf * width, width)
            terms = lax.dot_general(blocks, half, NT, preferred_element_type=F32)
            n = base_ref[i] * piece + g
            for b in range(per_leaf):
                p = place_ref[target_ref[n * per_leaf + b]]
                acc_ref[p] += terms[b * width:(b + 1) * width]

    if count == 1:
        step(inv_refs[0])
    else:
        for idx in range(count):
            pl.when(i == idx)(functools.partial(step, inv_refs[idx]))

    if not first:

        @pl.when(i == pl.num_programs(0) - 1)
        def _():
            def body(p, carry):
                sums_ref[p] = acc_ref[p].T[:columns]
                return carry

            lax.fori_loop(0, acc_ref.shape[0], body, 0)


def backward_kernel(group, per_leaf, target_ref, place_ref, r_ref, sent_ref, fwd_ref, inv_ref, blk_ref, out_ref):
    i = pl.program_id(0)
    for g in range(group):
        corr = None
        for b in range(per_leaf):
            k = (i * group + g) * per_leaf + b
            p = place_ref[target_ref[k]]
            term = lax.dot_general(sent_ref[p], blk_ref[g * per_leaf + b], NN, preferred_element_type=F32)
            corr = term if corr is None else corr + term
        back = (fwd_ref[g] - corr).astype(BF16)
        out_ref[g] = lax.dot_general(back, inv_ref[g], NN, preferred_element_type=F32)


def shift_pairs(size, shift):
    return [(i, (i + shift) % size) for i in range(size)]


def on_device(
    leaf_right, upper_right, leaf_inverse, upper_inverse, update_blocks, block_target, upper_place
):
    leaf_count, columns, width = leaf_right.shape
    block_count = update_blocks.shape[0]
    per_leaf = block_count // leaf_count
    upper_total = upper_place.shape[0]
    upper_rows = upper_right.shape[0]
    piece = leaf_inverse.shape[0]
    rhs_size = leaf_count // piece
    leaf_size = upper_total // upper_rows
    group = _group(piece)
    steps = leaf_count // group
    r = lax.axis_index("rhs")
    l = lax.axis_index("leaf")

    hier = rhs_size == 4
    if hier:
        from_x = lax.ppermute(leaf_inverse, "rhs", [(0, 2), (2, 0), (1, 3), (3, 1)])
        swap = [(0, 1), (1, 0), (2, 3), (3, 2)]
        inv_pieces = [leaf_inverse, from_x, lax.ppermute(leaf_inverse, "rhs", swap), None]
    else:
        inv_pieces = [leaf_inverse] + [
            lax.ppermute(leaf_inverse, "rhs", shift_pairs(rhs_size, s)) for s in range(1, rhs_size)
        ]

    target = block_target.reshape(block_count)
    place = upper_place.astype(jnp.int32)
    rr = jnp.reshape(r, (1,)).astype(jnp.int32)
    footprint = 4 * (upper_total * width * 128 * 4) + 4 * (piece * per_leaf * width * width * 2) + (8 << 20)
    grant = int(min(60 << 20, max(24 << 20, footprint)))
    params = pltpu.CompilerParams(
        dimension_semantics=("arbitrary",), vmem_limit_bytes=grant
    )

    def inv_map(i, t, q, rv):
        j = (i * group) // piece
        me = rv[0]
        if hier:
            slot = ((me % 2 + j % 2) % 2) * 2 + (me // 2 + j // 2) % 2
        else:
            slot = (me - j + rhs_size) % rhs_size
        return ((slot * piece + (i * group) % piece) // group, 0, 0)

    fwd_flops = 2 * leaf_count * columns * width * width * (1 + per_leaf)
    all_bytes = update_blocks.size * 2 + leaf_right.size * 8 + leaf_inverse.size * 2 * rhs_size
    cost = pl.CostEstimate(flops=fwd_flops, transcendentals=0, bytes_accessed=all_bytes)
    padded = -(-columns // 128) * 128
    if hier:
        slot_piece = [r, (r + 2) % 4, r + 1 - 2 * (r % 2), 3 - r]
        rest_order = [2, 1, 3]
    else:
        slot_piece = [(r - s_ + rhs_size) % rhs_size for s_ in range(rhs_size)]
        rest_order = list(range(1, rhs_size))

    def nat(i, t, q, bv):
        return (bv[i], 0, 0)

    def call(first, bases, inverses, extra):
        count = bases.shape[0]
        in_specs = [pl.BlockSpec((piece, columns, width), nat)]
        in_specs += [pl.BlockSpec((piece, width, width), lambda i, t, q, bv: (0, 0, 0))] * count
        in_specs += [pl.BlockSpec((piece * per_leaf, width, width), nat)]
        out_specs = [
            pl.BlockSpec((piece, columns, width), nat),
            pl.BlockSpec((upper_total, width, padded), lambda i, t, q, bv: (0, 0, 0)),
        ]
        out_shape = [
            jax.ShapeDtypeStruct((leaf_count, columns, width), F32),
            jax.ShapeDtypeStruct((upper_total, width, padded), F32),
        ]
        aliases = {}
        if not first:
            in_specs += [
                pl.BlockSpec((upper_total, width, padded), lambda i, t, q, bv: (0, 0, 0)),
                pl.BlockSpec(memory_space=pl.ANY),
            ]
            out_specs.append(pl.BlockSpec((upper_total, columns, width), lambda i, t, q, bv: (0, 0, 0)))
            out_shape.append(jax.ShapeDtypeStruct((upper_total, columns, width), F32))
            aliases = {5 + count: 1, 6 + count: 0}
        return pl.pallas_call(
            functools.partial(forward_kernel, per_leaf, piece, first, count),
            grid_spec=pltpu.PrefetchScalarGridSpec(
                num_scalar_prefetch=3,
                grid=(count,),
                in_specs=in_specs,
                out_specs=out_specs,
            ),
            out_shape=out_shape,
            input_output_aliases=aliases,
            compiler_params=params,
            cost_estimate=pl.CostEstimate(
                flops=fwd_flops * count // rhs_size,
                transcendentals=0,
                bytes_accessed=all_bytes * count // rhs_size,
            ),
        )(target, place, bases, leaf_right, *inverses, update_blocks, *extra)

    own_base = jnp.reshape(slot_piece[0], (1,)).astype(jnp.int32)
    fwd_own, acc_own = call(True, own_base, [leaf_inverse], [])
    if hier:
        held, _ = lax.optimization_barrier((from_x, acc_own))
        inv_pieces[3] = lax.ppermute(held, "rhs", swap)
    rest_bases = jnp.stack([slot_piece[s_] for s_ in rest_order]).astype(jnp.int32)
    leaf_forward, _, sums = call(False, rest_bases, [inv_pieces[s_] for s_ in rest_order], [acc_own, fwd_own])
    inv_stacked = jnp.concatenate(inv_pieces, axis=0)

    if leaf_size % 2 == 0:
        half_size = leaf_size // 2
        y = l % 2
        m = l // 2
        by_parity = sums.reshape(half_size, 2, upper_rows, columns, width)
        mine = lax.dynamic_index_in_dim(by_parity, y, axis=1, keepdims=False)
        theirs = lax.dynamic_index_in_dim(by_parity, 1 - y, axis=1, keepdims=False)
        pairs = [(i, i ^ 1) for i in range(leaf_size)]
        acc = mine + lax.ppermute(theirs, "leaf", pairs)
        own = lax.dynamic_index_in_dim(acc, m, axis=0, keepdims=False)
        for s_ in range(1, half_size):
            chunk = lax.dynamic_index_in_dim(acc, (m + s_) % half_size, axis=0, keepdims=False)
            own = own + lax.ppermute(chunk, "leaf", shift_pairs(leaf_size, 2 * s_))
    else:
        own = lax.dynamic_slice_in_dim(sums, l * upper_rows, upper_rows, 0)
        for s_ in range(1, leaf_size):
            dest = (l + s_) % leaf_size
            chunk = lax.dynamic_slice_in_dim(sums, dest * upper_rows, upper_rows, 0)
            own = own + lax.ppermute(chunk, "leaf", shift_pairs(leaf_size, s_))
    upper_rounded = (upper_right - own).astype(BF16)
    upper_half = jnp.einsum(
        "pcw,pvw->pcv", upper_rounded, upper_inverse, preferred_element_type=F32
    ).astype(BF16)
    upper_solution = jnp.einsum(
        "pcw,pwv->pcv", upper_half, upper_inverse, preferred_element_type=F32
    )
    sent = upper_solution.astype(BF16)
    sent_copies = jnp.broadcast_to(sent[None], (leaf_size,) + sent.shape)
    sent_all = lax.all_to_all(sent_copies, "leaf", 0, 0, tiled=False).reshape(
        (upper_total, columns, width)
    )

    leaf_solution = pl.pallas_call(
        functools.partial(backward_kernel, group, per_leaf),
        grid_spec=pltpu.PrefetchScalarGridSpec(
            num_scalar_prefetch=3,
            grid=(steps,),
            in_specs=[
                pl.BlockSpec((upper_total, columns, width), lambda i, t, q, rv: (0, 0, 0)),
                pl.BlockSpec((group, columns, width), lambda i, t, q, rv: (i, 0, 0)),
                pl.BlockSpec((group, width, width), inv_map),
                pl.BlockSpec((group * per_leaf, width, width), lambda i, t, q, rv: (i, 0, 0)),
            ],
            out_specs=pl.BlockSpec((group, columns, width), lambda i, t, q, rv: (i, 0, 0)),
        ),
        out_shape=jax.ShapeDtypeStruct((leaf_count, columns, width), F32),
        compiler_params=params,
        cost_estimate=cost,
    )(target, place, rr, sent_all, leaf_forward, inv_stacked, update_blocks)
    return (leaf_solution, upper_solution)


def solution(mesh):
    return jax.shard_map(
        on_device,
        mesh=mesh,
        in_specs=(
            P("leaf", "rhs", None),
            P("leaf", "rhs", None),
            P(("leaf", "rhs"), None, None),
            P("leaf", None, None),
            P("leaf", None, None),
            P("leaf", None),
            P(),
        ),
        out_specs=(P("leaf", "rhs", None), P("leaf", "rhs", None)),
        check_vma=False,
    )
```

```python
import functools

import jax
import jax.numpy as jnp
from jax import lax
from jax.experimental import pallas as pl
from jax.experimental.pallas import tpu as pltpu
from jax.sharding import PartitionSpec as P

F32 = jnp.float32
BF16 = jnp.bfloat16
NT = (((1,), (1,)), ((), ()))
NN = (((1,), (0,)), ((), ()))


def _group(count):
    for g in (8, 4, 2, 1):
        if count % g == 0:
            return g
    return 1


def forward_kernel(per_leaf, piece, first, count, target_ref, place_ref, base_ref, right_ref, *rest):
    inv_refs = rest[:count]
    blk_ref = rest[count]
    rest = rest[count + 1:]
    if first:
        fwd_ref, acc_ref = rest
    else:
        acc_in_ref, _, fwd_ref, acc_ref, sums_ref = rest
    i = pl.program_id(0)
    columns, width = right_ref.shape[1], right_ref.shape[2]
    padded = acc_ref.shape[2]

    @pl.when(i == 0)
    def _():
        if first:
            acc_ref[...] = jnp.zeros_like(acc_ref)
        else:
            acc_ref[...] = acc_in_ref[...]

    def step(inv_ref):
        for g in range(piece):
            rounded = right_ref[g].astype(BF16)
            forward = lax.dot_general(rounded, inv_ref[g], NT, preferred_element_type=F32)
            fwd_ref[g] = forward
            half = forward.astype(BF16)
            if padded > columns:
                half = jnp.concatenate([half, jnp.zeros((padded - columns, width), BF16)], axis=0)
            blocks = blk_ref[g * per_leaf:(g + 1) * per_leaf].reshape(per_leaf * width, width)
            terms = lax.dot_general(blocks, half, NT, preferred_element_type=F32)
            n = base_ref[i] * piece + g
            for b in range(per_leaf):
                p = place_ref[target_ref[n * per_leaf + b]]
                acc_ref[p] += terms[b * width:(b + 1) * width]

    if count == 1:
        step(inv_refs[0])
    else:
        for idx in range(count):
            pl.when(i == idx)(functools.partial(step, inv_refs[idx]))

    if not first:

        @pl.when(i == pl.num_programs(0) - 1)
        def _():
            def body(p, carry):
                sums_ref[p] = acc_ref[p].T[:columns]
                return carry

            lax.fori_loop(0, acc_ref.shape[0], body, 0)


def backward_kernel(group, per_leaf, target_ref, place_ref, r_ref, sent_ref, fwd_ref, inv_ref, blk_ref, out_ref):
    i = pl.program_id(0)
    for g in range(group):
        corr = None
        for b in range(per_leaf):
            k = (i * group + g) * per_leaf + b
            p = place_ref[target_ref[k]]
            term = lax.dot_general(sent_ref[p], blk_ref[g * per_leaf + b], NN, preferred_element_type=F32)
            corr = term if corr is None else corr + term
        back = (fwd_ref[g] - corr).astype(BF16)
        out_ref[g] = lax.dot_general(back, inv_ref[g], NN, preferred_element_type=F32)


def shift_pairs(size, shift):
    return [(i, (i + shift) % size) for i in range(size)]


def on_device(
    leaf_right, upper_right, leaf_inverse, upper_inverse, update_blocks, block_target, upper_place
):
    leaf_count, columns, width = leaf_right.shape
    block_count = update_blocks.shape[0]
    per_leaf = block_count // leaf_count
    upper_total = upper_place.shape[0]
    upper_rows = upper_right.shape[0]
    piece = leaf_inverse.shape[0]
    rhs_size = leaf_count // piece
    leaf_size = upper_total // upper_rows
    group = _group(piece)
    steps = leaf_count // group
    r = lax.axis_index("rhs")
    l = lax.axis_index("leaf")

    hier = rhs_size == 4
    if hier:
        from_x = lax.ppermute(leaf_inverse, "rhs", [(0, 2), (2, 0), (1, 3), (3, 1)])
        swap = [(0, 1), (1, 0), (2, 3), (3, 2)]
        inv_pieces = [leaf_inverse, from_x, lax.ppermute(leaf_inverse, "rhs", swap), None]
    else:
        inv_pieces = [leaf_inverse] + [
            lax.ppermute(leaf_inverse, "rhs", shift_pairs(rhs_size, s)) for s in range(1, rhs_size)
        ]

    target = block_target.reshape(block_count)
    place = upper_place.astype(jnp.int32)
    rr = jnp.reshape(r, (1,)).astype(jnp.int32)
    footprint = 4 * (upper_total * width * 128 * 4) + 4 * (piece * per_leaf * width * width * 2) + (8 << 20)
    grant = int(min(60 << 20, max(48 << 20, footprint)))
    params = pltpu.CompilerParams(
        dimension_semantics=("arbitrary",), vmem_limit_bytes=grant
    )

    def inv_map(i, t, q, rv):
        j = (i * group) // piece
        me = rv[0]
        if hier:
            slot = ((me % 2 + j % 2) % 2) * 2 + (me // 2 + j // 2) % 2
        else:
            slot = (me - j + rhs_size) % rhs_size
        return ((slot * piece + (i * group) % piece) // group, 0, 0)

    fwd_flops = 2 * leaf_count * columns * width * width * (1 + per_leaf)
    all_bytes = update_blocks.size * 2 + leaf_right.size * 8 + leaf_inverse.size * 2 * rhs_size
    cost = pl.CostEstimate(flops=fwd_flops, transcendentals=0, bytes_accessed=all_bytes)
    padded = -(-columns // 128) * 128
    if hier:
        slot_piece = [r, (r + 2) % 4, r + 1 - 2 * (r % 2), 3 - r]
        rest_order = [2, 1, 3]
    else:
        slot_piece = [(r - s_ + rhs_size) % rhs_size for s_ in range(rhs_size)]
        rest_order = list(range(1, rhs_size))

    def nat(i, t, q, bv):
        return (bv[i], 0, 0)

    def call(first, bases, inverses, extra):
        count = bases.shape[0]
        in_specs = [pl.BlockSpec((piece, columns, width), nat)]
        in_specs += [pl.BlockSpec((piece, width, width), lambda i, t, q, bv: (0, 0, 0))] * count
        in_specs += [pl.BlockSpec((piece * per_leaf, width, width), nat)]
        out_specs = [
            pl.BlockSpec((piece, columns, width), nat),
            pl.BlockSpec((upper_total, width, padded), lambda i, t, q, bv: (0, 0, 0)),
        ]
        out_shape = [
            jax.ShapeDtypeStruct((leaf_count, columns, width), F32),
            jax.ShapeDtypeStruct((upper_total, width, padded), F32),
        ]
        aliases = {}
        if not first:
            in_specs += [
                pl.BlockSpec((upper_total, width, padded), lambda i, t, q, bv: (0, 0, 0)),
                pl.BlockSpec(memory_space=pl.ANY),
            ]
            out_specs.append(pl.BlockSpec((upper_total, columns, width), lambda i, t, q, bv: (0, 0, 0)))
            out_shape.append(jax.ShapeDtypeStruct((upper_total, columns, width), F32))
            aliases = {5 + count: 1, 6 + count: 0}
        return pl.pallas_call(
            functools.partial(forward_kernel, per_leaf, piece, first, count),
            grid_spec=pltpu.PrefetchScalarGridSpec(
                num_scalar_prefetch=3,
                grid=(count,),
                in_specs=in_specs,
                out_specs=out_specs,
            ),
            out_shape=out_shape,
            input_output_aliases=aliases,
            compiler_params=params,
            cost_estimate=pl.CostEstimate(
                flops=fwd_flops * count // rhs_size,
                transcendentals=0,
                bytes_accessed=all_bytes * count // rhs_size,
            ),
        )(target, place, bases, leaf_right, *inverses, update_blocks, *extra)

    own_base = jnp.reshape(slot_piece[0], (1,)).astype(jnp.int32)
    fwd_own, acc_own = call(True, own_base, [leaf_inverse], [])
    if hier:
        held, _ = lax.optimization_barrier((from_x, acc_own))
        inv_pieces[3] = lax.ppermute(held, "rhs", swap)
    rest_bases = jnp.stack([slot_piece[s_] for s_ in rest_order]).astype(jnp.int32)
    leaf_forward, _, sums = call(False, rest_bases, [inv_pieces[s_] for s_ in rest_order], [acc_own, fwd_own])
    inv_stacked = jnp.concatenate(inv_pieces, axis=0)

    if leaf_size % 2 == 0:
        half_size = leaf_size // 2
        y = l % 2
        m = l // 2
        by_parity = sums.reshape(half_size, 2, upper_rows, columns, width)
        mine = lax.dynamic_index_in_dim(by_parity, y, axis=1, keepdims=False)
        theirs = lax.dynamic_index_in_dim(by_parity, 1 - y, axis=1, keepdims=False)
        pairs = [(i, i ^ 1) for i in range(leaf_size)]
        acc = mine + lax.ppermute(theirs, "leaf", pairs)
        own = lax.dynamic_index_in_dim(acc, m, axis=0, keepdims=False)
        for s_ in range(1, half_size):
            chunk = lax.dynamic_index_in_dim(acc, (m + s_) % half_size, axis=0, keepdims=False)
            own = own + lax.ppermute(chunk, "leaf", shift_pairs(leaf_size, 2 * s_))
    else:
        own = lax.dynamic_slice_in_dim(sums, l * upper_rows, upper_rows, 0)
        for s_ in range(1, leaf_size):
            dest = (l + s_) % leaf_size
            chunk = lax.dynamic_slice_in_dim(sums, dest * upper_rows, upper_rows, 0)
            own = own + lax.ppermute(chunk, "leaf", shift_pairs(leaf_size, s_))
    upper_rounded = (upper_right - own).astype(BF16)
    upper_half = jnp.einsum(
        "pcw,pvw->pcv", upper_rounded, upper_inverse, preferred_element_type=F32
    ).astype(BF16)
    upper_solution = jnp.einsum(
        "pcw,pwv->pcv", upper_half, upper_inverse, preferred_element_type=F32
    )
    sent = upper_solution.astype(BF16)
    sent_copies = jnp.broadcast_to(sent[None], (leaf_size,) + sent.shape)
    sent_all = lax.all_to_all(sent_copies, "leaf", 0, 0, tiled=False).reshape(
        (upper_total, columns, width)
    )

    leaf_solution = pl.pallas_call(
        functools.partial(backward_kernel, group, per_leaf),
        grid_spec=pltpu.PrefetchScalarGridSpec(
            num_scalar_prefetch=3,
            grid=(steps,),
            in_specs=[
                pl.BlockSpec((upper_total, columns, width), lambda i, t, q, rv: (0, 0, 0)),
                pl.BlockSpec((group, columns, width), lambda i, t, q, rv: (i, 0, 0)),
                pl.BlockSpec((group, width, width), inv_map),
                pl.BlockSpec((group * per_leaf, width, width), lambda i, t, q, rv: (i, 0, 0)),
            ],
            out_specs=pl.BlockSpec((group, columns, width), lambda i, t, q, rv: (i, 0, 0)),
        ),
        out_shape=jax.ShapeDtypeStruct((leaf_count, columns, width), F32),
        compiler_params=params,
        cost_estimate=cost,
    )(target, place, rr, sent_all, leaf_forward, inv_stacked, update_blocks)
    return (leaf_solution, upper_solution)


def solution(mesh):
    return jax.shard_map(
        on_device,
        mesh=mesh,
        in_specs=(
            P("leaf", "rhs", None),
            P("leaf", "rhs", None),
            P(("leaf", "rhs"), None, None),
            P("leaf", None, None),
            P("leaf", None, None),
            P("leaf", None),
            P(),
        ),
        out_specs=(P("leaf", "rhs", None), P("leaf", "rhs", None)),
        check_vma=False,
    )
```

```python
import functools

import jax
import jax.numpy as jnp
from jax import lax
from jax.experimental import pallas as pl
from jax.experimental.pallas import tpu as pltpu
from jax.sharding import PartitionSpec as P

F32 = jnp.float32
BF16 = jnp.bfloat16
NT = (((1,), (1,)), ((), ()))
NN = (((1,), (0,)), ((), ()))


def _group(count):
    for g in (8, 4, 2, 1):
        if count % g == 0:
            return g
    return 1


def forward_kernel(per_leaf, piece, first, count, target_ref, place_ref, base_ref, right_ref, *rest):
    inv_refs = rest[:count]
    blk_ref = rest[count]
    rest = rest[count + 1:]
    if first:
        fwd_ref, acc_ref = rest
    else:
        acc_in_ref, _, fwd_ref, acc_ref, sums_ref = rest
    i = pl.program_id(0)
    columns, width = right_ref.shape[1], right_ref.shape[2]
    padded = acc_ref.shape[2]

    @pl.when(i == 0)
    def _():
        if first:
            acc_ref[...] = jnp.zeros_like(acc_ref)
        else:
            acc_ref[...] = acc_in_ref[...]

    def step(inv_ref):
        for g in range(piece):
            rounded = right_ref[g].astype(BF16)
            forward = lax.dot_general(rounded, inv_ref[g], NT, preferred_element_type=F32)
            fwd_ref[g] = forward
            half = forward.astype(BF16)
            if padded > columns:
                half = jnp.concatenate([half, jnp.zeros((padded - columns, width), BF16)], axis=0)
            blocks = blk_ref[g * per_leaf:(g + 1) * per_leaf].reshape(per_leaf * width, width)
            terms = lax.dot_general(blocks, half, NT, preferred_element_type=F32)
            n = base_ref[i] * piece + g
            for b in range(per_leaf):
                p = place_ref[target_ref[n * per_leaf + b]]
                acc_ref[p] += terms[b * width:(b + 1) * width]

    if count == 1:
        step(inv_refs[0])
    else:
        for idx in range(count):
            pl.when(i == idx)(functools.partial(step, inv_refs[idx]))

    if not first:

        @pl.when(i == pl.num_programs(0) - 1)
        def _():
            def body(p, carry):
                sums_ref[p] = acc_ref[p].T[:columns]
                return carry

            lax.fori_loop(0, acc_ref.shape[0], body, 0)


def backward_kernel(group, per_leaf, target_ref, place_ref, r_ref, sent_ref, fwd_ref, inv_ref, blk_ref, out_ref):
    i = pl.program_id(0)
    for g in range(group):
        corr = None
        for b in range(per_leaf):
            k = (i * group + g) * per_leaf + b
            p = place_ref[target_ref[k]]
            term = lax.dot_general(sent_ref[p], blk_ref[g * per_leaf + b], NN, preferred_element_type=F32)
            corr = term if corr is None else corr + term
        back = (fwd_ref[g] - corr).astype(BF16)
        out_ref[g] = lax.dot_general(back, inv_ref[g], NN, preferred_element_type=F32)


def shift_pairs(size, shift):
    return [(i, (i + shift) % size) for i in range(size)]


def on_device(
    leaf_right, upper_right, leaf_inverse, upper_inverse, update_blocks, block_target, upper_place
):
    leaf_count, columns, width = leaf_right.shape
    block_count = update_blocks.shape[0]
    per_leaf = block_count // leaf_count
    upper_total = upper_place.shape[0]
    upper_rows = upper_right.shape[0]
    piece = leaf_inverse.shape[0]
    rhs_size = leaf_count // piece
    leaf_size = upper_total // upper_rows
    group = _group(piece)
    steps = leaf_count // group
    r = lax.axis_index("rhs")
    l = lax.axis_index("leaf")

    hier = rhs_size == 4
    if hier:
        from_x = lax.ppermute(leaf_inverse, "rhs", [(0, 2), (2, 0), (1, 3), (3, 1)])
        swap = [(0, 1), (1, 0), (2, 3), (3, 2)]
        inv_pieces = [leaf_inverse, from_x, lax.ppermute(leaf_inverse, "rhs", swap), None]
    else:
        inv_pieces = [leaf_inverse] + [
            lax.ppermute(leaf_inverse, "rhs", shift_pairs(rhs_size, s)) for s in range(1, rhs_size)
        ]

    target = block_target.reshape(block_count)
    place = upper_place.astype(jnp.int32)
    rr = jnp.reshape(r, (1,)).astype(jnp.int32)
    footprint = 4 * (upper_total * width * 128 * 4) + 4 * (piece * per_leaf * width * width * 2) + (8 << 20)
    grant = int(min(60 << 20, max(48 << 20, footprint)))
    params = pltpu.CompilerParams(
        dimension_semantics=("arbitrary",), vmem_limit_bytes=grant
    )

    def inv_map(i, t, q, rv):
        j = (i * group) // piece
        me = rv[0]
        if hier:
            slot = ((me % 2 + j % 2) % 2) * 2 + (me // 2 + j // 2) % 2
        else:
            slot = (me - j + rhs_size) % rhs_size
        return ((slot * piece + (i * group) % piece) // group, 0, 0)

    fwd_flops = 2 * leaf_count * columns * width * width * (1 + per_leaf)
    all_bytes = update_blocks.size * 2 + leaf_right.size * 8 + leaf_inverse.size * 2 * rhs_size
    cost = pl.CostEstimate(flops=fwd_flops, transcendentals=0, bytes_accessed=all_bytes)
    padded = -(-columns // 128) * 128
    if hier:
        slot_piece = [r, (r + 2) % 4, r + 1 - 2 * (r % 2), 3 - r]
        first_order = [0, 2]
        rest_order = [1, 3]
    else:
        slot_piece = [(r - s_ + rhs_size) % rhs_size for s_ in range(rhs_size)]
        first_order = [0]
        rest_order = list(range(1, rhs_size))

    def nat(i, t, q, bv):
        return (bv[i], 0, 0)

    def call(first, bases, inverses, extra):
        count = bases.shape[0]
        in_specs = [pl.BlockSpec((piece, columns, width), nat)]
        in_specs += [pl.BlockSpec((piece, width, width), lambda i, t, q, bv: (0, 0, 0))] * count
        in_specs += [pl.BlockSpec((piece * per_leaf, width, width), nat)]
        out_specs = [
            pl.BlockSpec((piece, columns, width), nat),
            pl.BlockSpec((upper_total, width, padded), lambda i, t, q, bv: (0, 0, 0)),
        ]
        out_shape = [
            jax.ShapeDtypeStruct((leaf_count, columns, width), F32),
            jax.ShapeDtypeStruct((upper_total, width, padded), F32),
        ]
        aliases = {}
        if not first:
            in_specs += [
                pl.BlockSpec((upper_total, width, padded), lambda i, t, q, bv: (0, 0, 0)),
                pl.BlockSpec(memory_space=pl.ANY),
            ]
            out_specs.append(pl.BlockSpec((upper_total, columns, width), lambda i, t, q, bv: (0, 0, 0)))
            out_shape.append(jax.ShapeDtypeStruct((upper_total, columns, width), F32))
            aliases = {5 + count: 1, 6 + count: 0}
        return pl.pallas_call(
            functools.partial(forward_kernel, per_leaf, piece, first, count),
            grid_spec=pltpu.PrefetchScalarGridSpec(
                num_scalar_prefetch=3,
                grid=(count,),
                in_specs=in_specs,
                out_specs=out_specs,
            ),
            out_shape=out_shape,
            input_output_aliases=aliases,
            compiler_params=params,
            cost_estimate=pl.CostEstimate(
                flops=fwd_flops * count // rhs_size,
                transcendentals=0,
                bytes_accessed=all_bytes * count // rhs_size,
            ),
        )(target, place, bases, leaf_right, *inverses, update_blocks, *extra)

    own_base = jnp.stack([slot_piece[s_] for s_ in first_order]).astype(jnp.int32)
    fwd_own, acc_own = call(True, own_base, [inv_pieces[s_] for s_ in first_order], [])
    if hier:
        held, _ = lax.optimization_barrier((from_x, acc_own))
        inv_pieces[3] = lax.ppermute(held, "rhs", swap)
    rest_bases = jnp.stack([slot_piece[s_] for s_ in rest_order]).astype(jnp.int32)
    leaf_forward, _, sums = call(False, rest_bases, [inv_pieces[s_] for s_ in rest_order], [acc_own, fwd_own])
    inv_stacked = jnp.concatenate(inv_pieces, axis=0)

    if leaf_size % 2 == 0:
        half_size = leaf_size // 2
        y = l % 2
        m = l // 2
        by_parity = sums.reshape(half_size, 2, upper_rows, columns, width)
        mine = lax.dynamic_index_in_dim(by_parity, y, axis=1, keepdims=False)
        theirs = lax.dynamic_index_in_dim(by_parity, 1 - y, axis=1, keepdims=False)
        pairs = [(i, i ^ 1) for i in range(leaf_size)]
        acc = mine + lax.ppermute(theirs, "leaf", pairs)
        own = lax.dynamic_index_in_dim(acc, m, axis=0, keepdims=False)
        for s_ in range(1, half_size):
            chunk = lax.dynamic_index_in_dim(acc, (m + s_) % half_size, axis=0, keepdims=False)
            own = own + lax.ppermute(chunk, "leaf", shift_pairs(leaf_size, 2 * s_))
    else:
        own = lax.dynamic_slice_in_dim(sums, l * upper_rows, upper_rows, 0)
        for s_ in range(1, leaf_size):
            dest = (l + s_) % leaf_size
            chunk = lax.dynamic_slice_in_dim(sums, dest * upper_rows, upper_rows, 0)
            own = own + lax.ppermute(chunk, "leaf", shift_pairs(leaf_size, s_))
    upper_rounded = (upper_right - own).astype(BF16)
    upper_half = jnp.einsum(
        "pcw,pvw->pcv", upper_rounded, upper_inverse, preferred_element_type=F32
    ).astype(BF16)
    upper_solution = jnp.einsum(
        "pcw,pwv->pcv", upper_half, upper_inverse, preferred_element_type=F32
    )
    sent = upper_solution.astype(BF16)
    sent_copies = jnp.broadcast_to(sent[None], (leaf_size,) + sent.shape)
    sent_all = lax.all_to_all(sent_copies, "leaf", 0, 0, tiled=False).reshape(
        (upper_total, columns, width)
    )

    leaf_solution = pl.pallas_call(
        functools.partial(backward_kernel, group, per_leaf),
        grid_spec=pltpu.PrefetchScalarGridSpec(
            num_scalar_prefetch=3,
            grid=(steps,),
            in_specs=[
                pl.BlockSpec((upper_total, columns, width), lambda i, t, q, rv: (0, 0, 0)),
                pl.BlockSpec((group, columns, width), lambda i, t, q, rv: (i, 0, 0)),
                pl.BlockSpec((group, width, width), inv_map),
                pl.BlockSpec((group * per_leaf, width, width), lambda i, t, q, rv: (i, 0, 0)),
            ],
            out_specs=pl.BlockSpec((group, columns, width), lambda i, t, q, rv: (i, 0, 0)),
        ),
        out_shape=jax.ShapeDtypeStruct((leaf_count, columns, width), F32),
        compiler_params=params,
        cost_estimate=cost,
    )(target, place, rr, sent_all, leaf_forward, inv_stacked, update_blocks)
    return (leaf_solution, upper_solution)


def solution(mesh):
    return jax.shard_map(
        on_device,
        mesh=mesh,
        in_specs=(
            P("leaf", "rhs", None),
            P("leaf", "rhs", None),
            P(("leaf", "rhs"), None, None),
            P("leaf", None, None),
            P("leaf", None, None),
            P("leaf", None),
            P(),
        ),
        out_specs=(P("leaf", "rhs", None), P("leaf", "rhs", None)),
        check_vma=False,
    )
```

```python
import functools

import jax
import jax.numpy as jnp
from jax import lax
from jax.experimental import pallas as pl
from jax.experimental.pallas import tpu as pltpu
from jax.sharding import PartitionSpec as P

F32 = jnp.float32
BF16 = jnp.bfloat16
NT = (((1,), (1,)), ((), ()))
NN = (((1,), (0,)), ((), ()))


def _group(count):
    for g in (8, 4, 2, 1):
        if count % g == 0:
            return g
    return 1


def forward_kernel(per_leaf, piece, first, count, target_ref, place_ref, base_ref, right_ref, *rest):
    inv_refs = rest[:count]
    blk_ref = rest[count]
    rest = rest[count + 1:]
    if first:
        fwd_ref, acc_ref = rest
    else:
        acc_in_ref, _, fwd_ref, acc_ref, sums_ref = rest
    i = pl.program_id(0)
    columns, width = right_ref.shape[1], right_ref.shape[2]
    padded = acc_ref.shape[2]

    @pl.when(i == 0)
    def _():
        if first:
            acc_ref[...] = jnp.zeros_like(acc_ref)
        else:
            acc_ref[...] = acc_in_ref[...]

    def step(inv_ref):
        for g in range(piece):
            rounded = right_ref[g].astype(BF16)
            forward = lax.dot_general(rounded, inv_ref[g], NT, preferred_element_type=F32)
            fwd_ref[g] = forward
            half = forward.astype(BF16)
            if padded > columns:
                half = jnp.concatenate([half, jnp.zeros((padded - columns, width), BF16)], axis=0)
            blocks = blk_ref[g * per_leaf:(g + 1) * per_leaf].reshape(per_leaf * width, width)
            terms = lax.dot_general(blocks, half, NT, preferred_element_type=F32)
            n = base_ref[i] * piece + g
            for b in range(per_leaf):
                p = place_ref[target_ref[n * per_leaf + b]]
                acc_ref[p] += terms[b * width:(b + 1) * width]

    if count == 1:
        step(inv_refs[0])
    else:
        for idx in range(count):
            pl.when(i == idx)(functools.partial(step, inv_refs[idx]))

    if not first:

        @pl.when(i == pl.num_programs(0) - 1)
        def _():
            def body(p, carry):
                sums_ref[p] = acc_ref[p].T[:columns]
                return carry

            lax.fori_loop(0, acc_ref.shape[0], body, 0)


def backward_kernel(group, per_leaf, target_ref, place_ref, r_ref, sent_ref, fwd_ref, inv_ref, blk_ref, out_ref):
    i = pl.program_id(0)
    for g in range(group):
        corr = None
        for b in range(per_leaf):
            k = (i * group + g) * per_leaf + b
            p = place_ref[target_ref[k]]
            term = lax.dot_general(sent_ref[p], blk_ref[g * per_leaf + b], NN, preferred_element_type=F32)
            corr = term if corr is None else corr + term
        back = (fwd_ref[g] - corr).astype(BF16)
        out_ref[g] = lax.dot_general(back, inv_ref[g], NN, preferred_element_type=F32)


def shift_pairs(size, shift):
    return [(i, (i + shift) % size) for i in range(size)]


def on_device(
    leaf_right, upper_right, leaf_inverse, upper_inverse, update_blocks, block_target, upper_place
):
    leaf_count, columns, width = leaf_right.shape
    block_count = update_blocks.shape[0]
    per_leaf = block_count // leaf_count
    upper_total = upper_place.shape[0]
    upper_rows = upper_right.shape[0]
    piece = leaf_inverse.shape[0]
    rhs_size = leaf_count // piece
    leaf_size = upper_total // upper_rows
    group = _group(piece)
    steps = leaf_count // group
    r = lax.axis_index("rhs")
    l = lax.axis_index("leaf")

    hier = rhs_size == 4
    if hier:
        x_pairs = [(0, 2), (2, 0), (1, 3), (3, 1)]
        cut = piece // 2
        from_x = jnp.concatenate(
            [lax.ppermute(leaf_inverse[:cut], "rhs", x_pairs), lax.ppermute(leaf_inverse[cut:], "rhs", x_pairs)],
            axis=0,
        )
        swap = [(0, 1), (1, 0), (2, 3), (3, 2)]
        inv_pieces = [leaf_inverse, from_x, lax.ppermute(leaf_inverse, "rhs", swap), None]
    else:
        inv_pieces = [leaf_inverse] + [
            lax.ppermute(leaf_inverse, "rhs", shift_pairs(rhs_size, s)) for s in range(1, rhs_size)
        ]

    target = block_target.reshape(block_count)
    place = upper_place.astype(jnp.int32)
    rr = jnp.reshape(r, (1,)).astype(jnp.int32)
    footprint = 4 * (upper_total * width * 128 * 4) + 4 * (piece * per_leaf * width * width * 2) + (8 << 20)
    grant = int(min(60 << 20, max(48 << 20, footprint)))
    params = pltpu.CompilerParams(
        dimension_semantics=("arbitrary",), vmem_limit_bytes=grant
    )

    def inv_map(i, t, q, rv):
        j = (i * group) // piece
        me = rv[0]
        if hier:
            slot = ((me % 2 + j % 2) % 2) * 2 + (me // 2 + j // 2) % 2
        else:
            slot = (me - j + rhs_size) % rhs_size
        return ((slot * piece + (i * group) % piece) // group, 0, 0)

    fwd_flops = 2 * leaf_count * columns * width * width * (1 + per_leaf)
    all_bytes = update_blocks.size * 2 + leaf_right.size * 8 + leaf_inverse.size * 2 * rhs_size
    cost = pl.CostEstimate(flops=fwd_flops, transcendentals=0, bytes_accessed=all_bytes)
    padded = -(-columns // 128) * 128
    if hier:
        slot_piece = [r, (r + 2) % 4, r + 1 - 2 * (r % 2), 3 - r]
        rest_order = [2, 1, 3]
    else:
        slot_piece = [(r - s_ + rhs_size) % rhs_size for s_ in range(rhs_size)]
        rest_order = list(range(1, rhs_size))

    def nat(i, t, q, bv):
        return (bv[i], 0, 0)

    def call(first, bases, inverses, extra):
        count = bases.shape[0]
        in_specs = [pl.BlockSpec((piece, columns, width), nat)]
        in_specs += [pl.BlockSpec((piece, width, width), lambda i, t, q, bv: (0, 0, 0))] * count
        in_specs += [pl.BlockSpec((piece * per_leaf, width, width), nat)]
        out_specs = [
            pl.BlockSpec((piece, columns, width), nat),
            pl.BlockSpec((upper_total, width, padded), lambda i, t, q, bv: (0, 0, 0)),
        ]
        out_shape = [
            jax.ShapeDtypeStruct((leaf_count, columns, width), F32),
            jax.ShapeDtypeStruct((upper_total, width, padded), F32),
        ]
        aliases = {}
        if not first:
            in_specs += [
                pl.BlockSpec((upper_total, width, padded), lambda i, t, q, bv: (0, 0, 0)),
                pl.BlockSpec(memory_space=pl.ANY),
            ]
            out_specs.append(pl.BlockSpec((upper_total, columns, width), lambda i, t, q, bv: (0, 0, 0)))
            out_shape.append(jax.ShapeDtypeStruct((upper_total, columns, width), F32))
            aliases = {5 + count: 1, 6 + count: 0}
        return pl.pallas_call(
            functools.partial(forward_kernel, per_leaf, piece, first, count),
            grid_spec=pltpu.PrefetchScalarGridSpec(
                num_scalar_prefetch=3,
                grid=(count,),
                in_specs=in_specs,
                out_specs=out_specs,
            ),
            out_shape=out_shape,
            input_output_aliases=aliases,
            compiler_params=params,
            cost_estimate=pl.CostEstimate(
                flops=fwd_flops * count // rhs_size,
                transcendentals=0,
                bytes_accessed=all_bytes * count // rhs_size,
            ),
        )(target, place, bases, leaf_right, *inverses, update_blocks, *extra)

    own_base = jnp.reshape(slot_piece[0], (1,)).astype(jnp.int32)
    fwd_own, acc_own = call(True, own_base, [leaf_inverse], [])
    if hier:
        held, _ = lax.optimization_barrier((from_x, acc_own))
        inv_pieces[3] = lax.ppermute(held, "rhs", swap)
    rest_bases = jnp.stack([slot_piece[s_] for s_ in rest_order]).astype(jnp.int32)
    leaf_forward, _, sums = call(False, rest_bases, [inv_pieces[s_] for s_ in rest_order], [acc_own, fwd_own])
    inv_stacked = jnp.concatenate(inv_pieces, axis=0)

    if leaf_size % 2 == 0:
        half_size = leaf_size // 2
        y = l % 2
        m = l // 2
        by_parity = sums.reshape(half_size, 2, upper_rows, columns, width)
        mine = lax.dynamic_index_in_dim(by_parity, y, axis=1, keepdims=False)
        theirs = lax.dynamic_index_in_dim(by_parity, 1 - y, axis=1, keepdims=False)
        pairs = [(i, i ^ 1) for i in range(leaf_size)]
        if half_size % 2 == 0:
            h = half_size // 2
            acc = mine + jnp.concatenate(
                [lax.ppermute(theirs[:h], "leaf", pairs), lax.ppermute(theirs[h:], "leaf", pairs)], axis=0
            )
        else:
            acc = mine + lax.ppermute(theirs, "leaf", pairs)
        own = lax.dynamic_index_in_dim(acc, m, axis=0, keepdims=False)
        for s_ in range(1, half_size):
            chunk = lax.dynamic_index_in_dim(acc, (m + s_) % half_size, axis=0, keepdims=False)
            own = own + lax.ppermute(chunk, "leaf", shift_pairs(leaf_size, 2 * s_))
    else:
        own = lax.dynamic_slice_in_dim(sums, l * upper_rows, upper_rows, 0)
        for s_ in range(1, leaf_size):
            dest = (l + s_) % leaf_size
            chunk = lax.dynamic_slice_in_dim(sums, dest * upper_rows, upper_rows, 0)
            own = own + lax.ppermute(chunk, "leaf", shift_pairs(leaf_size, s_))
    upper_rounded = (upper_right - own).astype(BF16)
    upper_half = jnp.einsum(
        "pcw,pvw->pcv", upper_rounded, upper_inverse, preferred_element_type=F32
    ).astype(BF16)
    upper_solution = jnp.einsum(
        "pcw,pwv->pcv", upper_half, upper_inverse, preferred_element_type=F32
    )
    sent = upper_solution.astype(BF16)
    sent_copies = jnp.broadcast_to(sent[None], (leaf_size,) + sent.shape)
    sent_all = lax.all_to_all(sent_copies, "leaf", 0, 0, tiled=False).reshape(
        (upper_total, columns, width)
    )

    leaf_solution = pl.pallas_call(
        functools.partial(backward_kernel, group, per_leaf),
        grid_spec=pltpu.PrefetchScalarGridSpec(
            num_scalar_prefetch=3,
            grid=(steps,),
            in_specs=[
                pl.BlockSpec((upper_total, columns, width), lambda i, t, q, rv: (0, 0, 0)),
                pl.BlockSpec((group, columns, width), lambda i, t, q, rv: (i, 0, 0)),
                pl.BlockSpec((group, width, width), inv_map),
                pl.BlockSpec((group * per_leaf, width, width), lambda i, t, q, rv: (i, 0, 0)),
            ],
            out_specs=pl.BlockSpec((group, columns, width), lambda i, t, q, rv: (i, 0, 0)),
        ),
        out_shape=jax.ShapeDtypeStruct((leaf_count, columns, width), F32),
        compiler_params=params,
        cost_estimate=cost,
    )(target, place, rr, sent_all, leaf_forward, inv_stacked, update_blocks)
    return (leaf_solution, upper_solution)


def solution(mesh):
    return jax.shard_map(
        on_device,
        mesh=mesh,
        in_specs=(
            P("leaf", "rhs", None),
            P("leaf", "rhs", None),
            P(("leaf", "rhs"), None, None),
            P("leaf", None, None),
            P("leaf", None, None),
            P("leaf", None),
            P(),
        ),
        out_specs=(P("leaf", "rhs", None), P("leaf", "rhs", None)),
        check_vma=False,
    )
```

```python
import functools

import jax
import jax.numpy as jnp
from jax import lax
from jax.experimental import pallas as pl
from jax.experimental.pallas import tpu as pltpu
from jax.sharding import PartitionSpec as P

F32 = jnp.float32
BF16 = jnp.bfloat16
NT = (((1,), (1,)), ((), ()))
NN = (((1,), (0,)), ((), ()))


def _group(count):
    for g in (8, 4, 2, 1):
        if count % g == 0:
            return g
    return 1


def forward_kernel(per_leaf, piece, first, count, target_ref, place_ref, base_ref, right_ref, *rest):
    inv_refs = rest[:count]
    blk_ref = rest[count]
    rest = rest[count + 1:]
    if first:
        fwd_ref, acc_ref = rest
    else:
        acc_in_ref, _, fwd_ref, acc_ref, sums_ref = rest
    i = pl.program_id(0)
    columns, width = right_ref.shape[1], right_ref.shape[2]
    padded = acc_ref.shape[2]

    @pl.when(i == 0)
    def _():
        if first:
            acc_ref[...] = jnp.zeros_like(acc_ref)
        else:
            acc_ref[...] = acc_in_ref[...]

    def step(inv_ref):
        for g in range(piece):
            rounded = right_ref[g].astype(BF16)
            forward = lax.dot_general(rounded, inv_ref[g], NT, preferred_element_type=F32)
            fwd_ref[g] = forward
            half = forward.astype(BF16)
            if padded > columns:
                half = jnp.concatenate([half, jnp.zeros((padded - columns, width), BF16)], axis=0)
            blocks = blk_ref[g * per_leaf:(g + 1) * per_leaf].reshape(per_leaf * width, width)
            terms = lax.dot_general(blocks, half, NT, preferred_element_type=F32)
            n = base_ref[i] * piece + g
            for b in range(per_leaf):
                p = place_ref[target_ref[n * per_leaf + b]]
                acc_ref[p] += terms[b * width:(b + 1) * width]

    if count == 1:
        step(inv_refs[0])
    else:
        for idx in range(count):
            pl.when(i == idx)(functools.partial(step, inv_refs[idx]))

    if not first:

        @pl.when(i == pl.num_programs(0) - 1)
        def _():
            def body(p, carry):
                sums_ref[p] = acc_ref[p].T[:columns]
                return carry

            lax.fori_loop(0, acc_ref.shape[0], body, 0)


def backward_kernel(group, per_leaf, target_ref, place_ref, r_ref, sent_ref, fwd_ref, inv_ref, blk_ref, out_ref):
    i = pl.program_id(0)
    for g in range(group):
        corr = None
        for b in range(per_leaf):
            k = (i * group + g) * per_leaf + b
            p = place_ref[target_ref[k]]
            term = lax.dot_general(sent_ref[p], blk_ref[g * per_leaf + b], NN, preferred_element_type=F32)
            corr = term if corr is None else corr + term
        back = (fwd_ref[g] - corr).astype(BF16)
        out_ref[g] = lax.dot_general(back, inv_ref[g], NN, preferred_element_type=F32)


def shift_pairs(size, shift):
    return [(i, (i + shift) % size) for i in range(size)]


def on_device(
    leaf_right, upper_right, leaf_inverse, upper_inverse, update_blocks, block_target, upper_place
):
    leaf_count, columns, width = leaf_right.shape
    block_count = update_blocks.shape[0]
    per_leaf = block_count // leaf_count
    upper_total = upper_place.shape[0]
    upper_rows = upper_right.shape[0]
    piece = leaf_inverse.shape[0]
    rhs_size = leaf_count // piece
    leaf_size = upper_total // upper_rows
    group = _group(piece)
    steps = leaf_count // group
    r = lax.axis_index("rhs")
    l = lax.axis_index("leaf")

    hier = rhs_size == 4
    if hier:
        from_x = lax.ppermute(leaf_inverse, "rhs", [(0, 2), (2, 0), (1, 3), (3, 1)])
        swap = [(0, 1), (1, 0), (2, 3), (3, 2)]
        inv_pieces = [leaf_inverse, from_x, lax.ppermute(leaf_inverse, "rhs", swap), None]
    else:
        inv_pieces = [leaf_inverse] + [
            lax.ppermute(leaf_inverse, "rhs", shift_pairs(rhs_size, s)) for s in range(1, rhs_size)
        ]

    target = block_target.reshape(block_count)
    place = upper_place.astype(jnp.int32)
    rr = jnp.reshape(r, (1,)).astype(jnp.int32)
    footprint = 4 * (upper_total * width * 128 * 4) + 4 * (piece * per_leaf * width * width * 2) + (8 << 20)
    grant = int(min(60 << 20, max(48 << 20, footprint)))
    params = pltpu.CompilerParams(
        dimension_semantics=("arbitrary",), vmem_limit_bytes=grant
    )

    def inv_map(i, t, q, rv):
        j = (i * group) // piece
        me = rv[0]
        if hier:
            slot = ((me % 2 + j % 2) % 2) * 2 + (me // 2 + j // 2) % 2
        else:
            slot = (me - j + rhs_size) % rhs_size
        return ((slot * piece + (i * group) % piece) // group, 0, 0)

    fwd_flops = 2 * leaf_count * columns * width * width * (1 + per_leaf)
    all_bytes = update_blocks.size * 2 + leaf_right.size * 8 + leaf_inverse.size * 2 * rhs_size
    cost = pl.CostEstimate(flops=fwd_flops, transcendentals=0, bytes_accessed=all_bytes)
    padded = -(-columns // 128) * 128
    if hier:
        slot_piece = [r, (r + 2) % 4, r + 1 - 2 * (r % 2), 3 - r]
        rest_order = [2, 1, 3]
    else:
        slot_piece = [(r - s_ + rhs_size) % rhs_size for s_ in range(rhs_size)]
        rest_order = list(range(1, rhs_size))

    def nat(i, t, q, bv):
        return (bv[i], 0, 0)

    def call(first, bases, inverses, extra):
        count = bases.shape[0]
        in_specs = [pl.BlockSpec((piece, columns, width), nat)]
        in_specs += [pl.BlockSpec((piece, width, width), lambda i, t, q, bv: (0, 0, 0))] * count
        in_specs += [pl.BlockSpec((piece * per_leaf, width, width), nat)]
        out_specs = [
            pl.BlockSpec((piece, columns, width), nat),
            pl.BlockSpec((upper_total, width, padded), lambda i, t, q, bv: (0, 0, 0)),
        ]
        out_shape = [
            jax.ShapeDtypeStruct((leaf_count, columns, width), F32),
            jax.ShapeDtypeStruct((upper_total, width, padded), F32),
        ]
        aliases = {}
        if not first:
            in_specs += [
                pl.BlockSpec((upper_total, width, padded), lambda i, t, q, bv: (0, 0, 0)),
                pl.BlockSpec(memory_space=pl.ANY),
            ]
            out_specs.append(pl.BlockSpec((upper_total, columns, width), lambda i, t, q, bv: (0, 0, 0)))
            out_shape.append(jax.ShapeDtypeStruct((upper_total, columns, width), F32))
            aliases = {5 + count: 1, 6 + count: 0}
        return pl.pallas_call(
            functools.partial(forward_kernel, per_leaf, piece, first, count),
            grid_spec=pltpu.PrefetchScalarGridSpec(
                num_scalar_prefetch=3,
                grid=(count,),
                in_specs=in_specs,
                out_specs=out_specs,
            ),
            out_shape=out_shape,
            input_output_aliases=aliases,
            compiler_params=params,
            cost_estimate=pl.CostEstimate(
                flops=fwd_flops * count // rhs_size,
                transcendentals=0,
                bytes_accessed=all_bytes * count // rhs_size,
            ),
        )(target, place, bases, leaf_right, *inverses, update_blocks, *extra)

    own_base = jnp.reshape(slot_piece[0], (1,)).astype(jnp.int32)
    fwd_own, acc_own = call(True, own_base, [leaf_inverse], [])
    if hier:
        held, _ = lax.optimization_barrier((from_x, acc_own))
        inv_pieces[3] = lax.ppermute(held, "rhs", swap)
    rest_bases = jnp.stack([slot_piece[s_] for s_ in rest_order]).astype(jnp.int32)
    leaf_forward, _, sums = call(False, rest_bases, [inv_pieces[s_] for s_ in rest_order], [acc_own, fwd_own])
    inv_stacked = jnp.concatenate(inv_pieces, axis=0)

    if leaf_size % 2 == 0:
        half_size = leaf_size // 2
        y = l % 2
        m = l // 2
        by_parity = sums.reshape(half_size, 2, upper_rows, columns, width)
        mine = lax.dynamic_index_in_dim(by_parity, y, axis=1, keepdims=False)
        theirs = lax.dynamic_index_in_dim(by_parity, 1 - y, axis=1, keepdims=False)
        pairs = [(i, i ^ 1) for i in range(leaf_size)]
        acc = mine + lax.ppermute(theirs, "leaf", pairs)
        own = lax.dynamic_index_in_dim(acc, m, axis=0, keepdims=False)
        for s_ in reversed(range(1, half_size)):
            chunk = lax.dynamic_index_in_dim(acc, (m + s_) % half_size, axis=0, keepdims=False)
            own = own + lax.ppermute(chunk, "leaf", shift_pairs(leaf_size, 2 * s_))
    else:
        own = lax.dynamic_slice_in_dim(sums, l * upper_rows, upper_rows, 0)
        for s_ in range(1, leaf_size):
            dest = (l + s_) % leaf_size
            chunk = lax.dynamic_slice_in_dim(sums, dest * upper_rows, upper_rows, 0)
            own = own + lax.ppermute(chunk, "leaf", shift_pairs(leaf_size, s_))
    upper_rounded = (upper_right - own).astype(BF16)
    upper_half = jnp.einsum(
        "pcw,pvw->pcv", upper_rounded, upper_inverse, preferred_element_type=F32
    ).astype(BF16)
    upper_solution = jnp.einsum(
        "pcw,pwv->pcv", upper_half, upper_inverse, preferred_element_type=F32
    )
    sent = upper_solution.astype(BF16)
    sent_copies = jnp.broadcast_to(sent[None], (leaf_size,) + sent.shape)
    sent_all = lax.all_to_all(sent_copies, "leaf", 0, 0, tiled=False).reshape(
        (upper_total, columns, width)
    )

    leaf_solution = pl.pallas_call(
        functools.partial(backward_kernel, group, per_leaf),
        grid_spec=pltpu.PrefetchScalarGridSpec(
            num_scalar_prefetch=3,
            grid=(steps,),
            in_specs=[
                pl.BlockSpec((upper_total, columns, width), lambda i, t, q, rv: (0, 0, 0)),
                pl.BlockSpec((group, columns, width), lambda i, t, q, rv: (i, 0, 0)),
                pl.BlockSpec((group, width, width), inv_map),
                pl.BlockSpec((group * per_leaf, width, width), lambda i, t, q, rv: (i, 0, 0)),
            ],
            out_specs=pl.BlockSpec((group, columns, width), lambda i, t, q, rv: (i, 0, 0)),
        ),
        out_shape=jax.ShapeDtypeStruct((leaf_count, columns, width), F32),
        compiler_params=params,
        cost_estimate=cost,
    )(target, place, rr, sent_all, leaf_forward, inv_stacked, update_blocks)
    return (leaf_solution, upper_solution)


def solution(mesh):
    return jax.shard_map(
        on_device,
        mesh=mesh,
        in_specs=(
            P("leaf", "rhs", None),
            P("leaf", "rhs", None),
            P(("leaf", "rhs"), None, None),
            P("leaf", None, None),
            P("leaf", None, None),
            P("leaf", None),
            P(),
        ),
        out_specs=(P("leaf", "rhs", None), P("leaf", "rhs", None)),
        check_vma=False,
    )
```
